512 devices in a mesh: seq: 64 (over y, z_lo, core), tp: 8 (over z_hi, x).
Axes of the slice: x: 4, y: 4, z: 16 (z_hi: 2, z_lo: 8; z = z_hi * 8 + z_lo), core: 2. Of those that a mesh axis runs over, the one named last changes fastest.
Arguments:
- tokens: bfloat16 [16384, 4096], P('seq', 'tp'), may hold values from -6 to 6
- ln_gain: float32 [4096], replicated, may hold values from 0.1 to 1.9
- ln_bias: float32 [4096], replicated, may hold values from -3 to 3
- w_qkv: bfloat16 [4096, 16, 3, 128], P('seq', 'tp'), may hold values from -3 to 3
- w_out: bfloat16 [16, 128, 4096], P('tp', None, 'seq'), may hold values from -0.25 to 0.25
- layer_scale: float32 [4096], P('tp'), may hold values from 0.5 to 2
- grids: int32 [14], replicated, may hold values from 24 to 40, as said below
- offsets: int32 [15], replicated, may hold values from 0 to 15302, as said below
Outputs:
- merged: bfloat16 [16384, 4, 4096], P('seq', None, 'tp')
The draws below stay inside these ranges and needn't reach their ends.
Inputs may be any that keep to these rules, and one draw needn't show every extreme that they name: `grids`: every side is even and some image has side exactly 40. Of images 2k and 2k + 1, one side is drawn and the other is the largest even side of at most 40 whose square keeps the two squares' sum within 2176. offsets[0] = 0 and offsets[s + 1] = offsets[s] + 5 + grids[s] * grids[s].
All inputs are finite; a program needn't handle non-finite values.
Results may differ from the reference program's by a relative error of at most 0.015.
Values may be sent and summed in bfloat16 or wider, within the bound.
No kernel may reach another device: no remote copies, remote signals or barrier semaphores. Data moves between devices by JAX's collectives and lax.ppermute only.
A program may use at most 64 MiB of HBM per device.

```python
import math
import jax
import jax.numpy as jnp
from jax import lax

D = 4096
H = 16
HD = 128
TOK_DEV = 256
G_MIN = 24
G_MAX = 40
HALO = 48
TOKENS = 16384
IMAGES = 14
REACH = 7
N_SEQ = 64
N_TP = 8


def image_layout(key):
    layout_key = jax.random.fold_in(key, 11)
    pair_count = IMAGES // 2
    half_first = jax.random.randint(jax.random.fold_in(layout_key, 1), (pair_count,), G_MIN // 2, G_MAX // 2 + 1)
    chosen = jax.random.randint(jax.random.fold_in(layout_key, 2), (), 0, pair_count)
    half_first = jnp.where(jnp.arange(pair_count) == chosen, G_MAX // 2, half_first)
    first_side = (2 * half_first).astype(jnp.int32)
    room = G_MIN * G_MIN + G_MAX * G_MAX - first_side * first_side
    candidates = (G_MIN + 2 * jnp.arange(1, (G_MAX - G_MIN) // 2 + 1)).astype(jnp.int32)
    fitting = (candidates[None, :] * candidates[None, :] <= room[:, None]).astype(jnp.int32)
    second_side = (G_MIN + 2 * jnp.sum(fitting, axis=1)).astype(jnp.int32)
    flipped = jax.random.randint(jax.random.fold_in(layout_key, 3), (pair_count,), 0, 2)
    side_a = jnp.where(flipped == 1, second_side, first_side)
    side_b = jnp.where(flipped == 1, first_side, second_side)
    sides = jnp.stack([side_a, side_b], axis=1).reshape(IMAGES).astype(jnp.int32)
    lengths = 5 + sides * sides
    starts = jnp.concatenate([jnp.zeros((1,), jnp.int32), jnp.cumsum(lengths).astype(jnp.int32)])
    return (sides, starts)


def draw_grids(key, part):
    return image_layout(key)[0]


def draw_offsets(key, part):
    return image_layout(key)[1]


def draw_w_qkv(key, part):
    normal_draw = jax.random.truncated_normal(key, -4.0, 4.0, (D, H, 3, HD), jnp.float32)
    query_part = normal_draw[:, :, 0] * (1.5 / D ** 0.5)
    key_part = normal_draw[:, :, 1] * (1.5 / D ** 0.5)
    value_part = normal_draw[:, :, 2] * (1.0 / D ** 0.5)
    stacked = jnp.stack([query_part, key_part, value_part], axis=2)
    return jnp.clip(stacked, -3.0, 3.0).astype(jnp.bfloat16)


def level_of(stream_key, extent, cuts, smallest, top_value):
    factor_of, own = 1.0, jax.random.fold_in(stream_key, 6)
    for axis_at, blocks in cuts:
        draws = jnp.exp(jax.random.uniform(jax.random.fold_in(own, axis_at), (blocks,), jnp.float32, smallest / len(cuts), top_value / len(cuts)))
        factor_of = factor_of * jnp.repeat(draws, extent[axis_at] // blocks).reshape([-1 if axis == axis_at else 1 for axis in range(len(extent))])
    return factor_of


def centred(key, shape, deviation, most, split=(), held_as=jnp.bfloat16):
    values = jax.random.normal(key, shape, jnp.float32) * deviation
    if len(split) > 0:
        values = level_of(key, shape, split, -0.22, 0.18) * values
    return jnp.clip(values, min=-most, max=most).astype(held_as)


def setup_inputs(seed: int = 0) -> dict:
    key_list = jax.random.split(jax.random.key(seed), 9)
    tokens = centred(key_list[0], (TOKENS, D), 1.0, 6.0, ((0, 64), (1, 8)))
    ln_gain = jnp.clip(1.0 + 0.18 * jax.random.normal(key_list[1], (D,), jnp.float32), 0.1, 1.9)
    ln_bias = centred(key_list[2], (D,), 0.3, 3.0, (), jnp.float32)
    w_qkv = draw_w_qkv(jax.random.fold_in(key_list[8], 71), 0)
    w_out = centred(key_list[4], (H, HD, D), (H * HD // 4) ** -0.5, 0.25, ((0, 8), (2, 64)))
    layer_scale = jnp.clip(jnp.exp(math.log(2.0) - 1.3862944 * jax.random.uniform(key_list[5], (D,), jnp.float32) ** level_of(key_list[5], (D,), ((0, 8),), -0.2, 0.2)), 0.5, 2.0)
    grids = draw_grids(jax.random.fold_in(key_list[8], 71), 0)
    offsets = draw_offsets(jax.random.fold_in(key_list[8], 71), 0)
    return {"tokens": tokens, "ln_gain": ln_gain, "ln_bias": ln_bias, "w_qkv": w_qkv, "w_out": w_out, "layer_scale": layer_scale, "grids": grids, "offsets": offsets}


def layout_rows(row_ids, offsets, grids, row_count):
    images = grids.shape[0]
    image_ends = offsets[1:]
    segment = lax.optimization_barrier(jnp.sum((row_ids[:, None] >= image_ends[None, :]).astype(jnp.int32), axis=1))
    inside = (row_ids >= 0) & (row_ids < row_count) & (segment < images)
    onehot = (jnp.minimum(segment, images - 1)[:, None] == jnp.arange(images, dtype=jnp.int32)[None, :]).astype(jnp.int32)
    image_start = lax.optimization_barrier(jnp.sum(onehot * offsets[None, :-1], axis=1))
    grid_side = lax.optimization_barrier(jnp.sum(onehot * grids[None, :], axis=1))
    position = row_ids - image_start
    is_patch = inside & (position >= 5)
    patch_index = jnp.maximum(position - 5, 0)
    return (segment, inside, is_patch, patch_index // grid_side, patch_index % grid_side, grid_side)

def rotate(vectors, is_patch, grid_row, grid_col, grid_side):
    quarter = vectors.shape[-1] // 4
    frequency = 2.0 * math.pi * jnp.power(100.0, -jnp.arange(quarter, dtype=jnp.float32) / quarter)
    side_float = grid_side.astype(jnp.float32)
    coord_row = (2 * grid_row + 1).astype(jnp.float32) / side_float - 1.0
    coord_col = (2 * grid_col + 1).astype(jnp.float32) / side_float - 1.0
    angles_row = jnp.where(is_patch[:, None], coord_row[:, None] * frequency[None, :], 0.0)
    angles_col = jnp.where(is_patch[:, None], coord_col[:, None] * frequency[None, :], 0.0)

    def rotate_half(block_vals, angles):
        first_half = block_vals[..., :quarter]
        second_half = block_vals[..., quarter:]
        cosine = jnp.cos(angles)[:, None, :]
        sine_part = jnp.sin(angles)[:, None, :]
        return jnp.concatenate([first_half * cosine - second_half * sine_part, second_half * cosine + first_half * sine_part], axis=-1)
    return jnp.concatenate([rotate_half(vectors[..., :2 * quarter], angles_row), rotate_half(vectors[..., 2 * quarter:], angles_col)], axis=-1)

def attend(query_matrix, block_of_keys, block_of_values, query_segment, query_inside, key_segment, key_inside):
    logit_scale_factor = 1.0 / math.sqrt(query_matrix.shape[-1])
    attention_logits = jnp.einsum('ecn,dcn->ced', query_matrix.astype(jnp.float32), block_of_keys.astype(jnp.float32)) * logit_scale_factor
    allowed = query_inside[:, None] & key_inside[None, :] & (query_segment[:, None] == key_segment[None, :])
    masked = jnp.where(allowed[None], attention_logits, -1e+30)
    row_max = lax.optimization_barrier(jnp.max(masked, axis=2, keepdims=True))
    exp_terms = jnp.where(allowed[None], jnp.exp(masked - row_max), 0.0)
    row_total = lax.optimization_barrier(jnp.sum(exp_terms, axis=2, keepdims=True))
    row_total = jnp.where(query_inside[None, :, None], row_total, 1.0)
    softmax_probabilities = (exp_terms / row_total).astype(jnp.bfloat16)
    attended_output = jnp.einsum('vgm,mvb->gvb', softmax_probabilities.astype(jnp.float32), block_of_values.astype(jnp.float32))
    attended_output = jnp.where(query_inside[:, None, None], attended_output, 0.0)
    return attended_output.astype(jnp.bfloat16)

def reference(tokens, ln_gain, ln_bias, w_qkv, w_out, layer_scale, grids, offsets):
    widened = tokens.astype(jnp.float32)
    average = lax.optimization_barrier(jnp.mean(widened, axis=-1, keepdims=True))
    spread_sq = lax.optimization_barrier(jnp.mean(jnp.square(widened - average), axis=-1, keepdims=True))
    normed = ((widened - average) * lax.rsqrt(spread_sq + 1e-06) * ln_gain + ln_bias).astype(jnp.bfloat16)
    qkv_sums = jnp.dot(normed, w_qkv.reshape(D, H * 3 * HD), preferred_element_type=jnp.float32).reshape(TOKENS, H, 3, HD)
    row_ids = jnp.arange(TOKENS, dtype=jnp.int32)
    segment, inside, is_patch, grid_row, grid_col, grid_side = layout_rows(row_ids, offsets, grids, TOKENS)
    query_matrix = rotate(qkv_sums[:, :, 0], is_patch, grid_row, grid_col, grid_side).astype(jnp.bfloat16)
    roped_keys = rotate(qkv_sums[:, :, 1], is_patch, grid_row, grid_col, grid_side).astype(jnp.bfloat16)
    values = qkv_sums[:, :, 2].astype(jnp.bfloat16)
    margin = REACH * TOK_DEV
    window = (2 * REACH + 1) * TOK_DEV
    padding = jnp.zeros((margin, H, HD), jnp.bfloat16)
    padded_keys = jnp.concatenate([padding, roped_keys, padding], axis=0)
    padded_values = jnp.concatenate([padding, values, padding], axis=0)

    def one_block(block):
        begin = (block * TOK_DEV).astype(jnp.int32)
        block_queries = lax.dynamic_slice_in_dim(query_matrix, begin, TOK_DEV, 0)
        block_keys = lax.dynamic_slice_in_dim(padded_keys, begin, window, 0)
        block_values = lax.dynamic_slice_in_dim(padded_values, begin, window, 0)
        query_rows = begin + jnp.arange(TOK_DEV, dtype=jnp.int32)
        key_rows = begin - margin + jnp.arange(window, dtype=jnp.int32)
        query_layout = layout_rows(query_rows, offsets, grids, TOKENS)
        key_layout = layout_rows(key_rows, offsets, grids, TOKENS)
        return attend(block_queries, block_keys, block_values, query_layout[0], query_layout[1], key_layout[0], key_layout[1])
    attended_output = lax.map(one_block, jnp.arange(N_SEQ, dtype=jnp.int32)).reshape(TOKENS, H, HD)
    group_heads = H // N_TP
    head_total = jnp.zeros((TOKENS, D), jnp.float32)
    for group in range(N_TP):
        share = jnp.dot(attended_output[:, group * group_heads:(group + 1) * group_heads].reshape(TOKENS, group_heads * HD), w_out[group * group_heads:(group + 1) * group_heads].reshape(group_heads * HD, D), preferred_element_type=jnp.float32)
        share = lax.optimization_barrier(share.astype(jnp.bfloat16)).astype(jnp.float32)
        head_total = head_total + share
    layer_out = (widened + layer_scale * head_total).astype(jnp.bfloat16)
    extended = jnp.concatenate([layer_out, jnp.zeros((HALO, D), jnp.bfloat16)], axis=0)
    is_corner = is_patch & (grid_row % 2 == 0) & (grid_col % 2 == 0)
    corner_index = jnp.stack([row_ids, row_ids + 1, row_ids + grid_side, row_ids + grid_side + 1], axis=1)
    corner_index = jnp.clip(corner_index, 0, TOKENS + HALO - 1).astype(jnp.int32)
    merged = jnp.take(extended, corner_index, axis=0)
    return jnp.where(is_corner[:, None, None], merged, jnp.zeros_like(merged))
```

```python
import functools
import math

import jax
import jax.numpy as jnp
from jax import lax
from jax.sharding import Mesh, PartitionSpec as P

HALO = 48
REACH = 7


def from_behind(shard, axis, by):
    count = lax.axis_size(axis)
    pairs = [(i, i + by) for i in range(count) if 0 <= i + by < count]
    return lax.ppermute(shard, axis, pairs)


def layout_rows(row_ids, offsets, grids, row_count):
    images = grids.shape[0]
    image_ends = offsets[1:]
    segment = jnp.sum((row_ids[:, None] >= image_ends[None, :]).astype(jnp.int32), axis=1)
    inside = (row_ids >= 0) & (row_ids < row_count) & (segment < images)
    onehot = (
        jnp.minimum(segment, images - 1)[:, None] == jnp.arange(images, dtype=jnp.int32)[None, :]
    ).astype(jnp.int32)
    image_start = jnp.sum(onehot * offsets[None, :-1], axis=1)
    grid_side = jnp.sum(onehot * grids[None, :], axis=1)
    position = row_ids - image_start
    is_patch = inside & (position >= 5)
    patch_index = jnp.maximum(position - 5, 0)
    return (segment, inside, is_patch, patch_index // grid_side, patch_index % grid_side, grid_side)


def rotate(vectors, is_patch, grid_row, grid_col, grid_side):
    quarter = vectors.shape[-1] // 4
    frequency = 2.0 * math.pi * jnp.power(100.0, -jnp.arange(quarter, dtype=jnp.float32) / quarter)
    side_float = grid_side.astype(jnp.float32)
    coord_row = (2 * grid_row + 1).astype(jnp.float32) / side_float - 1.0
    coord_col = (2 * grid_col + 1).astype(jnp.float32) / side_float - 1.0
    angles_row = jnp.where(is_patch[:, None], coord_row[:, None] * frequency[None, :], 0.0)
    angles_col = jnp.where(is_patch[:, None], coord_col[:, None] * frequency[None, :], 0.0)

    def rotate_half(block_vals, angles):
        first_half = block_vals[..., :quarter]
        second_half = block_vals[..., quarter:]
        cosine = jnp.cos(angles)[:, None, :]
        sine_part = jnp.sin(angles)[:, None, :]
        return jnp.concatenate(
            [
                first_half * cosine - second_half * sine_part,
                second_half * cosine + first_half * sine_part,
            ],
            axis=-1,
        )

    return jnp.concatenate(
        [
            rotate_half(vectors[..., : 2 * quarter], angles_row),
            rotate_half(vectors[..., 2 * quarter :], angles_col),
        ],
        axis=-1,
    )


def attend_blocks(query_matrix, kv_blocks, key_segment, key_inside, query_segment, query_inside):
    logit_scale_factor = 1.0 / math.sqrt(query_matrix.shape[-1])
    rows_here = query_matrix.shape[0]
    heads_here = query_matrix.shape[1]

    def block_scores(block_of_keys, segment_block, inside_block):
        attention_logits = (
            jnp.einsum(
                "ecn,dcn->ced", query_matrix, block_of_keys, preferred_element_type=jnp.float32
            )
            * logit_scale_factor
        )
        allowed = (
            query_inside[:, None]
            & inside_block[None, :]
            & (query_segment[:, None] == segment_block[None, :])
        )
        return (jnp.where(allowed[None], attention_logits, -1e30), allowed)

    def max_step(carry, input_block_rows):
        row_max, row_total = carry
        masked, allowed = block_scores(
            input_block_rows[0][:, 0], input_block_rows[1], input_block_rows[2]
        )
        new_max = jnp.maximum(row_max, jnp.max(masked, axis=2, keepdims=True))
        exp_terms = jnp.where(allowed[None], jnp.exp(masked - new_max), 0.0)
        row_total = row_total * jnp.exp(row_max - new_max) + jnp.sum(
            exp_terms, axis=2, keepdims=True
        )
        return ((new_max, row_total), None)

    start_max = jnp.full((heads_here, rows_here, 1), -1e30, jnp.float32)
    start_total = jnp.zeros((heads_here, rows_here, 1), jnp.float32)
    (row_max, row_total), _ = lax.scan(
        max_step, (start_max, start_total), (kv_blocks, key_segment, key_inside)
    )
    row_total = jnp.where(query_inside[None, :, None], row_total, 1.0)

    def sum_step(running, input_block_rows):
        masked, allowed = block_scores(
            input_block_rows[0][:, 0], input_block_rows[1], input_block_rows[2]
        )
        exp_terms = jnp.where(allowed[None], jnp.exp(masked - row_max), 0.0)
        softmax_probabilities = (exp_terms / row_total).astype(jnp.bfloat16)
        return (
            running
            + jnp.einsum(
                "vgm,mvb->gvb",
                softmax_probabilities,
                input_block_rows[0][:, 1],
                preferred_element_type=jnp.float32,
            ),
            None,
        )

    start_sum = jnp.zeros((rows_here, heads_here, query_matrix.shape[2]), jnp.float32)
    attended_output, _ = lax.scan(sum_step, start_sum, (kv_blocks, key_segment, key_inside))
    attended_output = jnp.where(query_inside[:, None, None], attended_output, 0.0)
    return attended_output.astype(jnp.bfloat16)


SEQ = ("y", "zl", "c")
TP = ("zh", "x")


def ring(shard, axis, size, by):
    return lax.ppermute(shard, axis, [(i, (i + by) % size) for i in range(size)])


def chain(shard, axis, size, by):
    pairs = [(i, i + by) for i in range(size) if 0 <= i + by < size]
    return lax.ppermute(shard, axis, pairs)


def body(sizes, tokens, ln_gain, ln_bias, w_qkv, w_out, layer_scale, grids, offsets):
    n_y, n_zl, n_c, n_zh, n_x = sizes
    n_seq = n_y * n_zl * n_c
    rows_here = tokens.shape[0]
    row_count = rows_here * n_seq
    c = lax.axis_index("c")
    zh = lax.axis_index("zh")
    x = lax.axis_index("x")
    seq_index = (lax.axis_index("y") * n_zl + lax.axis_index("zl")) * n_c + c
    first_row = seq_index * rows_here

    wq_mine = lax.all_gather(w_qkv, ("y", "zl"), axis=0, tiled=False)
    wo_mine = lax.all_gather(w_out, ("y", "zl"), axis=2, tiled=False)
    wq_other = ring(wq_mine, "c", n_c, 1)
    wo_other = ring(wo_mine, "c", n_c, 1)

    partner = ring(tokens, "zh", n_zh, 1)
    pair = jnp.stack([tokens, partner])
    received = [pair] + [ring(pair, "x", n_x, s) for s in range(1, n_x)]
    by_shift = jnp.stack(received)
    by_x = jnp.take(by_shift, (x - jnp.arange(n_x)) % n_x, axis=0)
    by_zh = jnp.where(zh == 0, by_x, by_x[:, ::-1])
    gathered = jnp.transpose(by_zh, (2, 1, 0, 3)).reshape(rows_here, -1)

    widened = gathered.astype(jnp.float32)
    average = jnp.mean(widened, axis=-1, keepdims=True)
    spread_sq = jnp.mean(jnp.square(widened - average), axis=-1, keepdims=True)
    normed = ((widened - average) * lax.rsqrt(spread_sq + 1e-06) * ln_gain + ln_bias).astype(
        jnp.bfloat16
    )
    normed_v = normed.reshape(rows_here, n_y * n_zl, n_c, -1)
    normed_mine = lax.dynamic_index_in_dim(normed_v, c, axis=2, keepdims=False)
    normed_other = lax.dynamic_index_in_dim(normed_v, 1 - c, axis=2, keepdims=False)
    qkv_sums = jnp.einsum(
        "tjd,jdhcf->thcf", normed_mine, wq_mine, preferred_element_type=jnp.float32
    ) + jnp.einsum("tjd,jdhcf->thcf", normed_other, wq_other, preferred_element_type=jnp.float32)
    row_ids = first_row + jnp.arange(rows_here, dtype=jnp.int32)
    segment, inside, is_patch, grid_row, grid_col, grid_side = layout_rows(
        row_ids, offsets, grids, row_count
    )
    query_matrix = rotate(qkv_sums[:, :, 0], is_patch, grid_row, grid_col, grid_side).astype(
        jnp.bfloat16
    )
    roped_keys = rotate(qkv_sums[:, :, 1], is_patch, grid_row, grid_col, grid_side).astype(
        jnp.bfloat16
    )
    values = qkv_sums[:, :, 2].astype(jnp.bfloat16)
    key_value = jnp.stack([roped_keys, values], axis=1)
    block_count = 2 * REACH + 1
    pieces = [None] * block_count
    pieces[REACH] = key_value
    from_left = key_value
    from_right = key_value
    for distance in range(1, REACH + 1):
        from_left = chain(from_left, SEQ, n_seq, 1)
        from_right = chain(from_right, SEQ, n_seq, -1)
        pieces[REACH - distance] = from_left
        pieces[REACH + distance] = from_right
    kv_blocks = jnp.stack(pieces, axis=0)
    key_rows = first_row - REACH * rows_here + jnp.arange(block_count * rows_here, dtype=jnp.int32)
    key_layout = layout_rows(key_rows, offsets, grids, row_count)
    key_segment = key_layout[0].reshape(block_count, rows_here)
    key_inside = key_layout[1].reshape(block_count, rows_here)
    attended_output = attend_blocks(
        query_matrix, kv_blocks, key_segment, key_inside, segment, inside
    )
    proj_mine = jnp.einsum(
        "thf,hfjd->tjd", attended_output, wo_mine, preferred_element_type=jnp.float32
    ).astype(jnp.bfloat16)
    proj_other = jnp.einsum(
        "thf,hfjd->tjd", attended_output, wo_other, preferred_element_type=jnp.float32
    ).astype(jnp.bfloat16)
    first_half = jnp.where(c == 0, proj_mine, proj_other)
    second_half = jnp.where(c == 0, proj_other, proj_mine)
    share = jnp.stack([first_half, second_half], axis=2).reshape(rows_here, n_zh, n_x, -1)

    total = lax.dynamic_index_in_dim(share, x, axis=2, keepdims=False).astype(jnp.float32)
    for s in range(1, n_x):
        outgoing = lax.dynamic_index_in_dim(share, (x + s) % n_x, axis=2, keepdims=False)
        total = total + ring(outgoing, "x", n_x, s).astype(jnp.float32)
    keep = lax.dynamic_index_in_dim(total, zh, axis=1, keepdims=False)
    give = lax.dynamic_index_in_dim(total, 1 - zh, axis=1, keepdims=False)
    head_share = keep + ring(give.astype(jnp.bfloat16), "zh", n_zh, 1).astype(jnp.float32)

    layer_out = (tokens.astype(jnp.float32) + layer_scale * head_share).astype(jnp.bfloat16)
    next_rows = chain(layer_out[:HALO], SEQ, n_seq, -1)
    extended = jnp.concatenate([layer_out, next_rows], axis=0)
    is_corner = is_patch & (grid_row % 2 == 0) & (grid_col % 2 == 0)
    local_ids = jnp.arange(rows_here, dtype=jnp.int32)
    corner_index = jnp.stack(
        [local_ids, local_ids + 1, local_ids + grid_side, local_ids + grid_side + 1], axis=1
    )
    corner_index = jnp.clip(corner_index, 0, extended.shape[0] - 1)
    merged = jnp.take(extended, corner_index, axis=0)
    return jnp.where(is_corner[:, None, None], merged, jnp.zeros_like(merged))


def solution(mesh):
    n_seq, n_tp = mesh.devices.shape
    n_c = 2
    n_y = 4
    n_zh = 2
    sizes = (n_y, n_seq // (n_y * n_c), n_c, n_zh, n_tp // n_zh)
    split = Mesh(mesh.devices.reshape(sizes), ("y", "zl", "c", "zh", "x"))
    placed = (
        P(SEQ, TP),
        P(),
        P(),
        P(SEQ, TP, None, None),
        P(TP, None, SEQ),
        P(TP),
        P(),
        P(),
    )
    return jax.shard_map(
        functools.partial(body, sizes),
        mesh=split,
        in_specs=placed,
        out_specs=P(SEQ, None, TP),
        check_vma=False,
    )
```

```python
import functools
import math

import jax
import jax.numpy as jnp
from jax import lax
from jax.sharding import Mesh, PartitionSpec as P

HALO = 48
REACH = 7


def from_behind(shard, axis, by):
    count = lax.axis_size(axis)
    pairs = [(i, i + by) for i in range(count) if 0 <= i + by < count]
    return lax.ppermute(shard, axis, pairs)


def layout_rows(row_ids, offsets, grids, row_count):
    images = grids.shape[0]
    image_ends = offsets[1:]
    segment = jnp.sum((row_ids[:, None] >= image_ends[None, :]).astype(jnp.int32), axis=1)
    inside = (row_ids >= 0) & (row_ids < row_count) & (segment < images)
    onehot = (
        jnp.minimum(segment, images - 1)[:, None] == jnp.arange(images, dtype=jnp.int32)[None, :]
    ).astype(jnp.int32)
    image_start = jnp.sum(onehot * offsets[None, :-1], axis=1)
    grid_side = jnp.sum(onehot * grids[None, :], axis=1)
    position = row_ids - image_start
    is_patch = inside & (position >= 5)
    patch_index = jnp.maximum(position - 5, 0)
    return (segment, inside, is_patch, patch_index // grid_side, patch_index % grid_side, grid_side)


def rotate(vectors, is_patch, grid_row, grid_col, grid_side):
    quarter = vectors.shape[-1] // 4
    frequency = 2.0 * math.pi * jnp.power(100.0, -jnp.arange(quarter, dtype=jnp.float32) / quarter)
    side_float = grid_side.astype(jnp.float32)
    coord_row = (2 * grid_row + 1).astype(jnp.float32) / side_float - 1.0
    coord_col = (2 * grid_col + 1).astype(jnp.float32) / side_float - 1.0
    angles_row = jnp.where(is_patch[:, None], coord_row[:, None] * frequency[None, :], 0.0)
    angles_col = jnp.where(is_patch[:, None], coord_col[:, None] * frequency[None, :], 0.0)

    def rotate_half(block_vals, angles):
        first_half = block_vals[..., :quarter]
        second_half = block_vals[..., quarter:]
        cosine = jnp.cos(angles)[:, None, :]
        sine_part = jnp.sin(angles)[:, None, :]
        return jnp.concatenate(
            [
                first_half * cosine - second_half * sine_part,
                second_half * cosine + first_half * sine_part,
            ],
            axis=-1,
        )

    return jnp.concatenate(
        [
            rotate_half(vectors[..., : 2 * quarter], angles_row),
            rotate_half(vectors[..., 2 * quarter :], angles_col),
        ],
        axis=-1,
    )


def attend_blocks(query_matrix, kv_blocks, key_segment, key_inside, query_segment, query_inside):
    logit_scale_factor = 1.0 / math.sqrt(query_matrix.shape[-1])
    rows_here = query_matrix.shape[0]
    heads_here = query_matrix.shape[1]

    def block_scores(block_of_keys, segment_block, inside_block):
        attention_logits = (
            jnp.einsum(
                "ecn,dcn->ced", query_matrix, block_of_keys, preferred_element_type=jnp.float32
            )
            * logit_scale_factor
        )
        allowed = (
            query_inside[:, None]
            & inside_block[None, :]
            & (query_segment[:, None] == segment_block[None, :])
        )
        return (jnp.where(allowed[None], attention_logits, -1e30), allowed)

    def max_step(carry, input_block_rows):
        row_max, row_total = carry
        masked, allowed = block_scores(
            input_block_rows[0][:, 0], input_block_rows[1], input_block_rows[2]
        )
        new_max = jnp.maximum(row_max, jnp.max(masked, axis=2, keepdims=True))
        exp_terms = jnp.where(allowed[None], jnp.exp(masked - new_max), 0.0)
        row_total = row_total * jnp.exp(row_max - new_max) + jnp.sum(
            exp_terms, axis=2, keepdims=True
        )
        return ((new_max, row_total), None)

    start_max = jnp.full((heads_here, rows_here, 1), -1e30, jnp.float32)
    start_total = jnp.zeros((heads_here, rows_here, 1), jnp.float32)
    (row_max, row_total), _ = lax.scan(
        max_step, (start_max, start_total), (kv_blocks, key_segment, key_inside)
    )
    row_total = jnp.where(query_inside[None, :, None], row_total, 1.0)

    def sum_step(running, input_block_rows):
        masked, allowed = block_scores(
            input_block_rows[0][:, 0], input_block_rows[1], input_block_rows[2]
        )
        exp_terms = jnp.where(allowed[None], jnp.exp(masked - row_max), 0.0)
        softmax_probabilities = (exp_terms / row_total).astype(jnp.bfloat16)
        return (
            running
            + jnp.einsum(
                "vgm,mvb->gvb",
                softmax_probabilities,
                input_block_rows[0][:, 1],
                preferred_element_type=jnp.float32,
            ),
            None,
        )

    start_sum = jnp.zeros((rows_here, heads_here, query_matrix.shape[2]), jnp.float32)
    attended_output, _ = lax.scan(sum_step, start_sum, (kv_blocks, key_segment, key_inside))
    attended_output = jnp.where(query_inside[:, None, None], attended_output, 0.0)
    return attended_output.astype(jnp.bfloat16)


SEQ = ("y", "zl", "c")
TP = ("zh", "x")


def ring(shard, axis, size, by):
    return lax.ppermute(shard, axis, [(i, (i + by) % size) for i in range(size)])


def chain(shard, axis, size, by):
    pairs = [(i, i + by) for i in range(size) if 0 <= i + by < size]
    return lax.ppermute(shard, axis, pairs)


def gather_seq_blocks(local, n_y, n_zl):
    zl = lax.axis_index("zl")
    y = lax.axis_index("y")
    left, right = local, local
    lefts, rights = [], []
    for _ in range(1, n_zl):
        left = chain(left, "zl", n_zl, 1)
        right = chain(right, "zl", n_zl, -1)
        lefts.append(left)
        rights.append(right)
    every = jnp.stack(lefts[::-1] + [local] + rights)
    line = lax.dynamic_slice_in_dim(every, n_zl - 1 - zl, n_zl, axis=0)
    by_shift = jnp.stack([line] + [ring(line, "y", n_y, s) for s in range(1, n_y)])
    by_y = jnp.take(by_shift, (y - jnp.arange(n_y)) % n_y, axis=0)
    return by_y.reshape(n_y * n_zl, *local.shape)


def body(sizes, tokens, ln_gain, ln_bias, w_qkv, w_out, layer_scale, grids, offsets):
    n_y, n_zl, n_c, n_zh, n_x = sizes
    n_seq = n_y * n_zl * n_c
    rows_here = tokens.shape[0]
    row_count = rows_here * n_seq
    c = lax.axis_index("c")
    zh = lax.axis_index("zh")
    x = lax.axis_index("x")
    seq_index = (lax.axis_index("y") * n_zl + lax.axis_index("zl")) * n_c + c
    first_row = seq_index * rows_here

    wq_mine = gather_seq_blocks(w_qkv, n_y, n_zl)
    wo_mine = jnp.transpose(gather_seq_blocks(w_out, n_y, n_zl), (1, 2, 0, 3))
    wq_other = ring(wq_mine, "c", n_c, 1)
    wo_other = ring(wo_mine, "c", n_c, 1)

    partner = ring(tokens, "zh", n_zh, 1)
    pair = jnp.stack([tokens, partner])
    received = [pair] + [ring(pair, "x", n_x, s) for s in range(1, n_x)]
    by_shift = jnp.stack(received)
    by_x = jnp.take(by_shift, (x - jnp.arange(n_x)) % n_x, axis=0)
    by_zh = jnp.where(zh == 0, by_x, by_x[:, ::-1])
    gathered = jnp.transpose(by_zh, (2, 1, 0, 3)).reshape(rows_here, -1)

    widened = gathered.astype(jnp.float32)
    average = jnp.mean(widened, axis=-1, keepdims=True)
    spread_sq = jnp.mean(jnp.square(widened - average), axis=-1, keepdims=True)
    normed = ((widened - average) * lax.rsqrt(spread_sq + 1e-06) * ln_gain + ln_bias).astype(
        jnp.bfloat16
    )
    normed_v = normed.reshape(rows_here, n_y * n_zl, n_c, -1)
    normed_mine = lax.dynamic_index_in_dim(normed_v, c, axis=2, keepdims=False)
    normed_other = lax.dynamic_index_in_dim(normed_v, 1 - c, axis=2, keepdims=False)
    qkv_sums = jnp.einsum(
        "tjd,jdhcf->thcf", normed_mine, wq_mine, preferred_element_type=jnp.float32
    ) + jnp.einsum("tjd,jdhcf->thcf", normed_other, wq_other, preferred_element_type=jnp.float32)
    row_ids = first_row + jnp.arange(rows_here, dtype=jnp.int32)
    segment, inside, is_patch, grid_row, grid_col, grid_side = layout_rows(
        row_ids, offsets, grids, row_count
    )
    query_matrix = rotate(qkv_sums[:, :, 0], is_patch, grid_row, grid_col, grid_side).astype(
        jnp.bfloat16
    )
    roped_keys = rotate(qkv_sums[:, :, 1], is_patch, grid_row, grid_col, grid_side).astype(
        jnp.bfloat16
    )
    values = qkv_sums[:, :, 2].astype(jnp.bfloat16)
    key_value = jnp.stack([roped_keys, values], axis=1)
    block_count = 2 * REACH + 1
    pieces = [None] * block_count
    pieces[REACH] = key_value
    from_left = key_value
    from_right = key_value
    for distance in range(1, REACH + 1):
        from_left = chain(from_left, SEQ, n_seq, 1)
        from_right = chain(from_right, SEQ, n_seq, -1)
        pieces[REACH - distance] = from_left
        pieces[REACH + distance] = from_right
    kv_blocks = jnp.stack(pieces, axis=0)
    key_rows = first_row - REACH * rows_here + jnp.arange(block_count * rows_here, dtype=jnp.int32)
    key_layout = layout_rows(key_rows, offsets, grids, row_count)
    key_segment = key_layout[0].reshape(block_count, rows_here)
    key_inside = key_layout[1].reshape(block_count, rows_here)
    attended_output = attend_blocks(
        query_matrix, kv_blocks, key_segment, key_inside, segment, inside
    )
    proj_mine = jnp.einsum(
        "thf,hfjd->tjd", attended_output, wo_mine, preferred_element_type=jnp.float32
    ).astype(jnp.bfloat16)
    proj_other = jnp.einsum(
        "thf,hfjd->tjd", attended_output, wo_other, preferred_element_type=jnp.float32
    ).astype(jnp.bfloat16)
    first_half = jnp.where(c == 0, proj_mine, proj_other)
    second_half = jnp.where(c == 0, proj_other, proj_mine)
    share = jnp.stack([first_half, second_half], axis=2).reshape(rows_here, n_zh, n_x, -1)

    total = lax.dynamic_index_in_dim(share, x, axis=2, keepdims=False).astype(jnp.float32)
    for s in range(1, n_x):
        outgoing = lax.dynamic_index_in_dim(share, (x + s) % n_x, axis=2, keepdims=False)
        total = total + ring(outgoing, "x", n_x, s).astype(jnp.float32)
    keep = lax.dynamic_index_in_dim(total, zh, axis=1, keepdims=False)
    give = lax.dynamic_index_in_dim(total, 1 - zh, axis=1, keepdims=False)
    head_share = keep + ring(give.astype(jnp.bfloat16), "zh", n_zh, 1).astype(jnp.float32)

    layer_out = (tokens.astype(jnp.float32) + layer_scale * head_share).astype(jnp.bfloat16)
    next_rows = chain(layer_out[:HALO], SEQ, n_seq, -1)
    extended = jnp.concatenate([layer_out, next_rows], axis=0)
    is_corner = is_patch & (grid_row % 2 == 0) & (grid_col % 2 == 0)
    local_ids = jnp.arange(rows_here, dtype=jnp.int32)
    corner_index = jnp.stack(
        [local_ids, local_ids + 1, local_ids + grid_side, local_ids + grid_side + 1], axis=1
    )
    corner_index = jnp.clip(corner_index, 0, extended.shape[0] - 1)
    merged = jnp.take(extended, corner_index, axis=0)
    return jnp.where(is_corner[:, None, None], merged, jnp.zeros_like(merged))


def solution(mesh):
    n_seq, n_tp = mesh.devices.shape
    n_c = 2
    n_y = 4
    n_zh = 2
    sizes = (n_y, n_seq // (n_y * n_c), n_c, n_zh, n_tp // n_zh)
    split = Mesh(mesh.devices.reshape(sizes), ("y", "zl", "c", "zh", "x"))
    placed = (
        P(SEQ, TP),
        P(),
        P(),
        P(SEQ, TP, None, None),
        P(TP, None, SEQ),
        P(TP),
        P(),
        P(),
    )
    return jax.shard_map(
        functools.partial(body, sizes),
        mesh=split,
        in_specs=placed,
        out_specs=P(SEQ, None, TP),
        check_vma=False,
    )
```

```python
import functools
import math

import jax
import jax.numpy as jnp
from jax import lax
from jax.sharding import Mesh, PartitionSpec as P

HALO = 48
REACH = 7


def from_behind(shard, axis, by):
    count = lax.axis_size(axis)
    pairs = [(i, i + by) for i in range(count) if 0 <= i + by < count]
    return lax.ppermute(shard, axis, pairs)


def layout_rows(row_ids, offsets, grids, row_count):
    images = grids.shape[0]
    image_ends = offsets[1:]
    segment = jnp.sum((row_ids[:, None] >= image_ends[None, :]).astype(jnp.int32), axis=1)
    inside = (row_ids >= 0) & (row_ids < row_count) & (segment < images)
    onehot = (
        jnp.minimum(segment, images - 1)[:, None] == jnp.arange(images, dtype=jnp.int32)[None, :]
    ).astype(jnp.int32)
    image_start = jnp.sum(onehot * offsets[None, :-1], axis=1)
    grid_side = jnp.sum(onehot * grids[None, :], axis=1)
    position = row_ids - image_start
    is_patch = inside & (position >= 5)
    patch_index = jnp.maximum(position - 5, 0)
    return (segment, inside, is_patch, patch_index // grid_side, patch_index % grid_side, grid_side)


def rotate(vectors, is_patch, grid_row, grid_col, grid_side):
    quarter = vectors.shape[-1] // 4
    frequency = 2.0 * math.pi * jnp.power(100.0, -jnp.arange(quarter, dtype=jnp.float32) / quarter)
    side_float = grid_side.astype(jnp.float32)
    coord_row = (2 * grid_row + 1).astype(jnp.float32) / side_float - 1.0
    coord_col = (2 * grid_col + 1).astype(jnp.float32) / side_float - 1.0
    angles_row = jnp.where(is_patch[:, None], coord_row[:, None] * frequency[None, :], 0.0)
    angles_col = jnp.where(is_patch[:, None], coord_col[:, None] * frequency[None, :], 0.0)

    def rotate_half(block_vals, angles):
        first_half = block_vals[..., :quarter]
        second_half = block_vals[..., quarter:]
        cosine = jnp.cos(angles)[:, None, :]
        sine_part = jnp.sin(angles)[:, None, :]
        return jnp.concatenate(
            [
                first_half * cosine - second_half * sine_part,
                second_half * cosine + first_half * sine_part,
            ],
            axis=-1,
        )

    return jnp.concatenate(
        [
            rotate_half(vectors[..., : 2 * quarter], angles_row),
            rotate_half(vectors[..., 2 * quarter :], angles_col),
        ],
        axis=-1,
    )


def attend_all(query_matrix, block_of_keys, block_of_values, query_segment, query_inside, key_segment, key_inside):
    logit_scale_factor = 1.0 / math.sqrt(query_matrix.shape[-1])
    attention_logits = (
        jnp.einsum("ecn,dcn->ced", query_matrix, block_of_keys, preferred_element_type=jnp.float32)
        * logit_scale_factor
    )
    allowed = (
        query_inside[:, None]
        & key_inside[None, :]
        & (query_segment[:, None] == key_segment[None, :])
    )
    masked = jnp.where(allowed[None], attention_logits, -1e30)
    row_max = jnp.max(masked, axis=2, keepdims=True)
    exp_terms = jnp.where(allowed[None], jnp.exp(masked - row_max), 0.0)
    row_total = jnp.sum(exp_terms, axis=2, keepdims=True)
    row_total = jnp.where(query_inside[None, :, None], row_total, 1.0)
    softmax_probabilities = (exp_terms / row_total).astype(jnp.bfloat16)
    attended_output = jnp.einsum(
        "vgm,mvb->gvb", softmax_probabilities, block_of_values, preferred_element_type=jnp.float32
    )
    attended_output = jnp.where(query_inside[:, None, None], attended_output, 0.0)
    return attended_output.astype(jnp.bfloat16)


SEQ = ("y", "zl", "c")
TP = ("zh", "x")


def ring(shard, axis, size, by):
    return lax.ppermute(shard, axis, [(i, (i + by) % size) for i in range(size)])


def chain(shard, axis, size, by):
    pairs = [(i, i + by) for i in range(size) if 0 <= i + by < size]
    return lax.ppermute(shard, axis, pairs)


def gather_seq_blocks(local, n_y, n_zl):
    zl = lax.axis_index("zl")
    y = lax.axis_index("y")
    left, right = local, local
    lefts, rights = [], []
    for _ in range(1, n_zl):
        left = chain(left, "zl", n_zl, 1)
        right = chain(right, "zl", n_zl, -1)
        lefts.append(left)
        rights.append(right)
    every = jnp.stack(lefts[::-1] + [local] + rights)
    line = lax.dynamic_slice_in_dim(every, n_zl - 1 - zl, n_zl, axis=0)
    by_shift = jnp.stack([line] + [ring(line, "y", n_y, s) for s in range(1, n_y)])
    by_y = jnp.take(by_shift, (y - jnp.arange(n_y)) % n_y, axis=0)
    return by_y.reshape(n_y * n_zl, *local.shape)


def body(sizes, tokens, ln_gain, ln_bias, w_qkv, w_out, layer_scale, grids, offsets):
    n_y, n_zl, n_c, n_zh, n_x = sizes
    n_seq = n_y * n_zl * n_c
    rows_here = tokens.shape[0]
    row_count = rows_here * n_seq
    c = lax.axis_index("c")
    zh = lax.axis_index("zh")
    x = lax.axis_index("x")
    seq_index = (lax.axis_index("y") * n_zl + lax.axis_index("zl")) * n_c + c
    first_row = seq_index * rows_here

    both = jnp.concatenate([w_qkv.reshape(-1), w_out.reshape(-1)])
    both_mine = gather_seq_blocks(both, n_y, n_zl)
    both_other = ring(both_mine, "c", n_c, 1)
    split_at = w_qkv.size
    n_j = n_y * n_zl

    def unpack(gathered):
        wq = gathered[:, :split_at].reshape(n_j, *w_qkv.shape)
        wo = jnp.transpose(gathered[:, split_at:].reshape(n_j, *w_out.shape), (1, 2, 0, 3))
        return wq, wo

    wq_mine, wo_mine = unpack(both_mine)
    wq_other, wo_other = unpack(both_other)

    partner = ring(tokens, "zh", n_zh, 1)
    pair = jnp.stack([tokens, partner])
    received = [pair] + [ring(pair, "x", n_x, s) for s in range(1, n_x)]
    by_shift = jnp.stack(received)
    by_x = jnp.take(by_shift, (x - jnp.arange(n_x)) % n_x, axis=0)
    by_zh = jnp.where(zh == 0, by_x, by_x[:, ::-1])
    gathered = jnp.transpose(by_zh, (2, 1, 0, 3)).reshape(rows_here, -1)

    widened = gathered.astype(jnp.float32)
    average = jnp.mean(widened, axis=-1, keepdims=True)
    spread_sq = jnp.mean(jnp.square(widened - average), axis=-1, keepdims=True)
    normed = ((widened - average) * lax.rsqrt(spread_sq + 1e-06) * ln_gain + ln_bias).astype(
        jnp.bfloat16
    )
    normed_v = normed.reshape(rows_here, n_y * n_zl, n_c, -1)
    normed_mine = lax.dynamic_index_in_dim(normed_v, c, axis=2, keepdims=False)
    normed_other = lax.dynamic_index_in_dim(normed_v, 1 - c, axis=2, keepdims=False)
    qkv_sums = jnp.einsum(
        "tjd,jdhcf->thcf", normed_mine, wq_mine, preferred_element_type=jnp.float32
    ) + jnp.einsum("tjd,jdhcf->thcf", normed_other, wq_other, preferred_element_type=jnp.float32)
    row_ids = first_row + jnp.arange(rows_here, dtype=jnp.int32)
    segment, inside, is_patch, grid_row, grid_col, grid_side = layout_rows(
        row_ids, offsets, grids, row_count
    )
    query_matrix = rotate(qkv_sums[:, :, 0], is_patch, grid_row, grid_col, grid_side).astype(
        jnp.bfloat16
    )
    roped_keys = rotate(qkv_sums[:, :, 1], is_patch, grid_row, grid_col, grid_side).astype(
        jnp.bfloat16
    )
    values = qkv_sums[:, :, 2].astype(jnp.bfloat16)
    key_value = jnp.stack([roped_keys, values], axis=1)
    block_count = 2 * REACH + 1
    pieces = [None] * block_count
    pieces[REACH] = key_value
    from_left = key_value
    from_right = key_value
    for distance in range(1, REACH + 1):
        from_left = chain(from_left, SEQ, n_seq, 1)
        from_right = chain(from_right, SEQ, n_seq, -1)
        pieces[REACH - distance] = from_left
        pieces[REACH + distance] = from_right
    kv_all = jnp.concatenate(pieces, axis=0)
    key_rows = first_row - REACH * rows_here + jnp.arange(block_count * rows_here, dtype=jnp.int32)
    key_layout = layout_rows(key_rows, offsets, grids, row_count)
    attended_output = attend_all(
        query_matrix, kv_all[:, 0], kv_all[:, 1], segment, inside, key_layout[0], key_layout[1]
    )
    proj_mine = jnp.einsum(
        "thf,hfjd->tjd", attended_output, wo_mine, preferred_element_type=jnp.float32
    ).astype(jnp.bfloat16)
    proj_other = jnp.einsum(
        "thf,hfjd->tjd", attended_output, wo_other, preferred_element_type=jnp.float32
    ).astype(jnp.bfloat16)
    first_half = jnp.where(c == 0, proj_mine, proj_other)
    second_half = jnp.where(c == 0, proj_other, proj_mine)
    share = jnp.stack([first_half, second_half], axis=2).reshape(rows_here, n_zh, n_x, -1)

    total = lax.dynamic_index_in_dim(share, x, axis=2, keepdims=False).astype(jnp.float32)
    for s in range(1, n_x):
        outgoing = lax.dynamic_index_in_dim(share, (x + s) % n_x, axis=2, keepdims=False)
        total = total + ring(outgoing, "x", n_x, s).astype(jnp.float32)
    keep = lax.dynamic_index_in_dim(total, zh, axis=1, keepdims=False)
    give = lax.dynamic_index_in_dim(total, 1 - zh, axis=1, keepdims=False)
    head_share = keep + ring(give.astype(jnp.bfloat16), "zh", n_zh, 1).astype(jnp.float32)

    layer_out = (tokens.astype(jnp.float32) + layer_scale * head_share).astype(jnp.bfloat16)
    next_rows = chain(layer_out[:HALO], SEQ, n_seq, -1)
    extended = jnp.concatenate([layer_out, next_rows], axis=0)
    is_corner = is_patch & (grid_row % 2 == 0) & (grid_col % 2 == 0)
    local_ids = jnp.arange(rows_here, dtype=jnp.int32)
    corner_index = jnp.stack(
        [local_ids, local_ids + 1, local_ids + grid_side, local_ids + grid_side + 1], axis=1
    )
    corner_index = jnp.clip(corner_index, 0, extended.shape[0] - 1)
    merged = jnp.take(extended, corner_index, axis=0)
    return jnp.where(is_corner[:, None, None], merged, jnp.zeros_like(merged))


def solution(mesh):
    n_seq, n_tp = mesh.devices.shape
    n_c = 2
    n_y = 4
    n_zh = 2
    sizes = (n_y, n_seq // (n_y * n_c), n_c, n_zh, n_tp // n_zh)
    split = Mesh(mesh.devices.reshape(sizes), ("y", "zl", "c", "zh", "x"))
    placed = (
        P(SEQ, TP),
        P(),
        P(),
        P(SEQ, TP, None, None),
        P(TP, None, SEQ),
        P(TP),
        P(),
        P(),
    )
    return jax.shard_map(
        functools.partial(body, sizes),
        mesh=split,
        in_specs=placed,
        out_specs=P(SEQ, None, TP),
        check_vma=False,
    )
```

```python
import functools
import math

import jax
import jax.numpy as jnp
from jax import lax
from jax.sharding import Mesh, PartitionSpec as P

HALO = 48
REACH = 7


def from_behind(shard, axis, by):
    count = lax.axis_size(axis)
    pairs = [(i, i + by) for i in range(count) if 0 <= i + by < count]
    return lax.ppermute(shard, axis, pairs)


def layout_rows(row_ids, offsets, grids, row_count):
    images = grids.shape[0]
    image_ends = offsets[1:]
    segment = jnp.sum((row_ids[:, None] >= image_ends[None, :]).astype(jnp.int32), axis=1)
    inside = (row_ids >= 0) & (row_ids < row_count) & (segment < images)
    onehot = (
        jnp.minimum(segment, images - 1)[:, None] == jnp.arange(images, dtype=jnp.int32)[None, :]
    ).astype(jnp.int32)
    image_start = jnp.sum(onehot * offsets[None, :-1], axis=1)
    grid_side = jnp.sum(onehot * grids[None, :], axis=1)
    position = row_ids - image_start
    is_patch = inside & (position >= 5)
    patch_index = jnp.maximum(position - 5, 0)
    return (segment, inside, is_patch, patch_index // grid_side, patch_index % grid_side, grid_side)


def rotate(vectors, is_patch, grid_row, grid_col, grid_side):
    quarter = vectors.shape[-1] // 4
    frequency = 2.0 * math.pi * jnp.power(100.0, -jnp.arange(quarter, dtype=jnp.float32) / quarter)
    side_float = grid_side.astype(jnp.float32)
    coord_row = (2 * grid_row + 1).astype(jnp.float32) / side_float - 1.0
    coord_col = (2 * grid_col + 1).astype(jnp.float32) / side_float - 1.0
    angles_row = jnp.where(is_patch[:, None], coord_row[:, None] * frequency[None, :], 0.0)
    angles_col = jnp.where(is_patch[:, None], coord_col[:, None] * frequency[None, :], 0.0)

    def rotate_half(block_vals, angles):
        first_half = block_vals[..., :quarter]
        second_half = block_vals[..., quarter:]
        cosine = jnp.cos(angles)[:, None, :]
        sine_part = jnp.sin(angles)[:, None, :]
        return jnp.concatenate(
            [
                first_half * cosine - second_half * sine_part,
                second_half * cosine + first_half * sine_part,
            ],
            axis=-1,
        )

    return jnp.concatenate(
        [
            rotate_half(vectors[..., : 2 * quarter], angles_row),
            rotate_half(vectors[..., 2 * quarter :], angles_col),
        ],
        axis=-1,
    )


def attend_all(query_matrix, block_of_keys, block_of_values, query_segment, query_inside, key_segment, key_inside):
    logit_scale_factor = 1.0 / math.sqrt(query_matrix.shape[-1])
    attention_logits = (
        jnp.einsum("ecn,dcn->ced", query_matrix, block_of_keys, preferred_element_type=jnp.float32)
        * logit_scale_factor
    )
    allowed = (
        query_inside[:, None]
        & key_inside[None, :]
        & (query_segment[:, None] == key_segment[None, :])
    )
    masked = jnp.where(allowed[None], attention_logits, -1e30)
    row_max = jnp.max(masked, axis=2, keepdims=True)
    exp_terms = jnp.where(allowed[None], jnp.exp(masked - row_max), 0.0)
    row_total = jnp.sum(exp_terms, axis=2, keepdims=True)
    row_total = jnp.where(query_inside[None, :, None], row_total, 1.0)
    softmax_probabilities = (exp_terms / row_total).astype(jnp.bfloat16)
    attended_output = jnp.einsum(
        "vgm,mvb->gvb", softmax_probabilities, block_of_values, preferred_element_type=jnp.float32
    )
    attended_output = jnp.where(query_inside[:, None, None], attended_output, 0.0)
    return attended_output.astype(jnp.bfloat16)


SEQ = ("y", "zl", "c")
TP = ("zh", "x")


def ring(shard, axis, size, by):
    return lax.ppermute(shard, axis, [(i, (i + by) % size) for i in range(size)])


def chain(shard, axis, size, by):
    pairs = [(i, i + by) for i in range(size) if 0 <= i + by < size]
    return lax.ppermute(shard, axis, pairs)


def everyone(block, axis, size):
    repeated = jnp.broadcast_to(block[None], (size, *block.shape))
    return lax.all_to_all(repeated, axis, 0, 0, tiled=True)


def gather_seq_blocks(local, n_y, n_zl):
    line = everyone(local, "zl", n_zl)
    return everyone(line, "y", n_y).reshape(n_y * n_zl, *local.shape)


def body(sizes, tokens, ln_gain, ln_bias, w_qkv, w_out, layer_scale, grids, offsets):
    n_y, n_zl, n_c, n_zh, n_x = sizes
    n_seq = n_y * n_zl * n_c
    rows_here = tokens.shape[0]
    row_count = rows_here * n_seq
    c = lax.axis_index("c")
    zh = lax.axis_index("zh")
    x = lax.axis_index("x")
    seq_index = (lax.axis_index("y") * n_zl + lax.axis_index("zl")) * n_c + c
    first_row = seq_index * rows_here

    wq_local = w_qkv.reshape(w_qkv.shape[0], -1)
    wo_local = w_out.reshape(-1, w_out.shape[-1])
    wq_mine = gather_seq_blocks(wq_local, n_y, n_zl)
    wo_mine = gather_seq_blocks(wo_local, n_y, n_zl)
    wq_other = ring(wq_mine, "c", n_c, 1)
    wo_other = ring(wo_mine, "c", n_c, 1)

    partner = ring(tokens, "zh", n_zh, 1)
    pair = jnp.stack([tokens, partner])
    by_x = everyone(pair, "x", n_x).reshape(n_x, *pair.shape)
    by_zh = jnp.where(zh == 0, by_x, by_x[:, ::-1])
    gathered = jnp.transpose(by_zh, (2, 1, 0, 3)).reshape(rows_here, -1)

    widened = gathered.astype(jnp.float32)
    average = jnp.mean(widened, axis=-1, keepdims=True)
    spread_sq = jnp.mean(jnp.square(widened - average), axis=-1, keepdims=True)
    normed = ((widened - average) * lax.rsqrt(spread_sq + 1e-06) * ln_gain + ln_bias).astype(
        jnp.bfloat16
    )
    normed_v = normed.reshape(rows_here, n_y * n_zl, n_c, -1)
    normed_mine = lax.dynamic_index_in_dim(normed_v, c, axis=2, keepdims=False)
    normed_other = lax.dynamic_index_in_dim(normed_v, 1 - c, axis=2, keepdims=False)
    qkv_sums = (
        jnp.einsum("tjd,jdo->to", normed_mine, wq_mine, preferred_element_type=jnp.float32)
        + jnp.einsum("tjd,jdo->to", normed_other, wq_other, preferred_element_type=jnp.float32)
    ).reshape(rows_here, *w_qkv.shape[1:])
    row_ids = first_row + jnp.arange(rows_here, dtype=jnp.int32)
    segment, inside, is_patch, grid_row, grid_col, grid_side = layout_rows(
        row_ids, offsets, grids, row_count
    )
    query_matrix = rotate(qkv_sums[:, :, 0], is_patch, grid_row, grid_col, grid_side).astype(
        jnp.bfloat16
    )
    roped_keys = rotate(qkv_sums[:, :, 1], is_patch, grid_row, grid_col, grid_side).astype(
        jnp.bfloat16
    )
    values = qkv_sums[:, :, 2].astype(jnp.bfloat16)
    key_value = jnp.stack([roped_keys, values], axis=1)
    block_count = 2 * REACH + 1
    behind = key_value[None]
    ahead = key_value[None]
    width = 1
    while width <= REACH:
        behind = jnp.concatenate([chain(behind, SEQ, n_seq, width), behind], axis=0)
        ahead = jnp.concatenate([ahead, chain(ahead, SEQ, n_seq, -width)], axis=0)
        width *= 2
    kv_all = jnp.concatenate(
        [behind[behind.shape[0] - 1 - REACH :], ahead[1 : REACH + 1]], axis=0
    ).reshape(block_count * rows_here, *key_value.shape[1:])
    key_rows = first_row - REACH * rows_here + jnp.arange(block_count * rows_here, dtype=jnp.int32)
    key_layout = layout_rows(key_rows, offsets, grids, row_count)
    attended_output = attend_all(
        query_matrix, kv_all[:, 0], kv_all[:, 1], segment, inside, key_layout[0], key_layout[1]
    )
    attended_flat = attended_output.reshape(rows_here, -1)
    proj_mine = jnp.einsum(
        "tk,jkd->tjd", attended_flat, wo_mine, preferred_element_type=jnp.float32
    ).astype(jnp.bfloat16)
    proj_other = jnp.einsum(
        "tk,jkd->tjd", attended_flat, wo_other, preferred_element_type=jnp.float32
    ).astype(jnp.bfloat16)
    first_half = jnp.where(c == 0, proj_mine, proj_other)
    second_half = jnp.where(c == 0, proj_other, proj_mine)
    share = jnp.stack([first_half, second_half], axis=2).reshape(rows_here, n_zh, n_x, -1)

    by_target = jnp.transpose(share, (2, 0, 1, 3))
    from_peers = lax.all_to_all(by_target, "x", 0, 0, tiled=True)
    total = jnp.sum(from_peers.astype(jnp.float32), axis=0)
    keep = lax.dynamic_index_in_dim(total, zh, axis=1, keepdims=False)
    give = lax.dynamic_index_in_dim(total, 1 - zh, axis=1, keepdims=False)
    head_share = keep + ring(give.astype(jnp.bfloat16), "zh", n_zh, 1).astype(jnp.float32)

    layer_out = (tokens.astype(jnp.float32) + layer_scale * head_share).astype(jnp.bfloat16)
    next_rows = chain(layer_out[:HALO], SEQ, n_seq, -1)
    extended = jnp.concatenate([layer_out, next_rows], axis=0)
    is_corner = is_patch & (grid_row % 2 == 0) & (grid_col % 2 == 0)
    local_ids = jnp.arange(rows_here, dtype=jnp.int32)
    corner_index = jnp.stack(
        [local_ids, local_ids + 1, local_ids + grid_side, local_ids + grid_side + 1], axis=1
    )
    corner_index = jnp.clip(corner_index, 0, extended.shape[0] - 1)
    merged = jnp.take(extended, corner_index, axis=0)
    return jnp.where(is_corner[:, None, None], merged, jnp.zeros_like(merged))


def solution(mesh):
    n_seq, n_tp = mesh.devices.shape
    n_c = 2
    n_y = 4
    n_zh = 2
    sizes = (n_y, n_seq // (n_y * n_c), n_c, n_zh, n_tp // n_zh)
    split = Mesh(mesh.devices.reshape(sizes), ("y", "zl", "c", "zh", "x"))
    placed = (
        P(SEQ, TP),
        P(),
        P(),
        P(SEQ, TP, None, None),
        P(TP, None, SEQ),
        P(TP),
        P(),
        P(),
    )
    return jax.shard_map(
        functools.partial(body, sizes),
        mesh=split,
        in_specs=placed,
        out_specs=P(SEQ, None, TP),
        check_vma=False,
    )
```

```python
import functools
import math

import jax
import jax.numpy as jnp
from jax import lax
from jax.sharding import Mesh, PartitionSpec as P

HALO = 48
REACH = 7


def from_behind(shard, axis, by):
    count = lax.axis_size(axis)
    pairs = [(i, i + by) for i in range(count) if 0 <= i + by < count]
    return lax.ppermute(shard, axis, pairs)


def layout_rows(row_ids, offsets, grids, row_count):
    images = grids.shape[0]
    image_ends = offsets[1:]
    segment = jnp.sum((row_ids[:, None] >= image_ends[None, :]).astype(jnp.int32), axis=1)
    inside = (row_ids >= 0) & (row_ids < row_count) & (segment < images)
    onehot = (
        jnp.minimum(segment, images - 1)[:, None] == jnp.arange(images, dtype=jnp.int32)[None, :]
    ).astype(jnp.int32)
    image_start = jnp.sum(onehot * offsets[None, :-1], axis=1)
    grid_side = jnp.sum(onehot * grids[None, :], axis=1)
    position = row_ids - image_start
    is_patch = inside & (position >= 5)
    patch_index = jnp.maximum(position - 5, 0)
    return (segment, inside, is_patch, patch_index // grid_side, patch_index % grid_side, grid_side)


def rotate(vectors, is_patch, grid_row, grid_col, grid_side):
    quarter = vectors.shape[-1] // 4
    frequency = 2.0 * math.pi * jnp.power(100.0, -jnp.arange(quarter, dtype=jnp.float32) / quarter)
    side_float = grid_side.astype(jnp.float32)
    coord_row = (2 * grid_row + 1).astype(jnp.float32) / side_float - 1.0
    coord_col = (2 * grid_col + 1).astype(jnp.float32) / side_float - 1.0
    angles_row = jnp.where(is_patch[:, None], coord_row[:, None] * frequency[None, :], 0.0)
    angles_col = jnp.where(is_patch[:, None], coord_col[:, None] * frequency[None, :], 0.0)

    def rotate_half(block_vals, angles):
        first_half = block_vals[..., :quarter]
        second_half = block_vals[..., quarter:]
        cosine = jnp.cos(angles)[:, None, :]
        sine_part = jnp.sin(angles)[:, None, :]
        return jnp.concatenate(
            [
                first_half * cosine - second_half * sine_part,
                second_half * cosine + first_half * sine_part,
            ],
            axis=-1,
        )

    return jnp.concatenate(
        [
            rotate_half(vectors[..., : 2 * quarter], angles_row),
            rotate_half(vectors[..., 2 * quarter :], angles_col),
        ],
        axis=-1,
    )


def attend_all(query_matrix, block_of_keys, block_of_values, query_segment, query_inside, key_segment, key_inside):
    logit_scale_factor = 1.0 / math.sqrt(query_matrix.shape[-1])
    attention_logits = (
        jnp.einsum("ecn,dcn->ced", query_matrix, block_of_keys, preferred_element_type=jnp.float32)
        * logit_scale_factor
    )
    allowed = (
        query_inside[:, None]
        & key_inside[None, :]
        & (query_segment[:, None] == key_segment[None, :])
    )
    masked = jnp.where(allowed[None], attention_logits, -1e30)
    row_max = jnp.max(masked, axis=2, keepdims=True)
    exp_terms = jnp.where(allowed[None], jnp.exp(masked - row_max), 0.0)
    row_total = jnp.sum(exp_terms, axis=2, keepdims=True)
    row_total = jnp.where(query_inside[None, :, None], row_total, 1.0)
    softmax_probabilities = (exp_terms / row_total).astype(jnp.bfloat16)
    attended_output = jnp.einsum(
        "vgm,mvb->gvb", softmax_probabilities, block_of_values, preferred_element_type=jnp.float32
    )
    attended_output = jnp.where(query_inside[:, None, None], attended_output, 0.0)
    return attended_output.astype(jnp.bfloat16)


SEQ = ("y", "zl", "c")
TP = ("zh", "x")


def ring(shard, axis, size, by):
    return lax.ppermute(shard, axis, [(i, (i + by) % size) for i in range(size)])


def chain(shard, axis, size, by):
    pairs = [(i, i + by) for i in range(size) if 0 <= i + by < size]
    return lax.ppermute(shard, axis, pairs)


def everyone(block, axis, size):
    repeated = jnp.broadcast_to(block[None], (size, *block.shape))
    return lax.all_to_all(repeated, axis, 0, 0, tiled=True)


def gather_seq_blocks(local, n_y, n_zl):
    line = everyone(local, "zl", n_zl)
    return everyone(line, "y", n_y).reshape(n_y * n_zl, *local.shape)


def body(sizes, tokens, ln_gain, ln_bias, w_qkv, w_out, layer_scale, grids, offsets):
    n_y, n_zl, n_c, n_zh, n_x = sizes
    n_seq = n_y * n_zl * n_c
    rows_here = tokens.shape[0]
    row_count = rows_here * n_seq
    c = lax.axis_index("c")
    zh = lax.axis_index("zh")
    x = lax.axis_index("x")
    seq_index = (lax.axis_index("y") * n_zl + lax.axis_index("zl")) * n_c + c
    first_row = seq_index * rows_here

    wq_local = w_qkv.reshape(w_qkv.shape[0], -1)
    wo_local = w_out.reshape(-1, w_out.shape[-1])
    wq_mine = gather_seq_blocks(wq_local, n_y, n_zl)
    wo_mine = gather_seq_blocks(wo_local, n_y, n_zl)
    wq_other = ring(wq_mine, "c", n_c, 1)
    wo_other = ring(wo_mine, "c", n_c, 1)

    partner = ring(tokens, "zh", n_zh, 1)
    pair = jnp.stack([tokens, partner])
    by_x = everyone(pair, "x", n_x).reshape(n_x, *pair.shape)
    by_zh = jnp.where(zh == 0, by_x, by_x[:, ::-1])
    gathered = jnp.transpose(by_zh, (2, 1, 0, 3)).reshape(rows_here, -1)

    widened = gathered.astype(jnp.float32)
    average = jnp.mean(widened, axis=-1, keepdims=True)
    spread_sq = jnp.mean(jnp.square(widened - average), axis=-1, keepdims=True)
    normed = ((widened - average) * lax.rsqrt(spread_sq + 1e-06) * ln_gain + ln_bias).astype(
        jnp.bfloat16
    )
    normed_v = normed.reshape(rows_here, n_y * n_zl, n_c, -1)
    normed_mine = lax.dynamic_index_in_dim(normed_v, c, axis=2, keepdims=False)
    normed_other = lax.dynamic_index_in_dim(normed_v, 1 - c, axis=2, keepdims=False)
    qkv_sums = (
        jnp.einsum("tjd,jdo->to", normed_mine, wq_mine, preferred_element_type=jnp.float32)
        + jnp.einsum("tjd,jdo->to", normed_other, wq_other, preferred_element_type=jnp.float32)
    ).reshape(rows_here, *w_qkv.shape[1:])
    row_ids = first_row + jnp.arange(rows_here, dtype=jnp.int32)
    segment, inside, is_patch, grid_row, grid_col, grid_side = layout_rows(
        row_ids, offsets, grids, row_count
    )
    query_matrix = rotate(qkv_sums[:, :, 0], is_patch, grid_row, grid_col, grid_side).astype(
        jnp.bfloat16
    )
    roped_keys = rotate(qkv_sums[:, :, 1], is_patch, grid_row, grid_col, grid_side).astype(
        jnp.bfloat16
    )
    values = qkv_sums[:, :, 2].astype(jnp.bfloat16)
    key_value = jnp.stack([roped_keys, values], axis=1)
    block_count = 2 * REACH + 1
    behind = [key_value]
    ahead = [key_value]
    for _ in range(REACH):
        behind.insert(0, chain(behind[0], SEQ, n_seq, 1))
        ahead.append(chain(ahead[-1], SEQ, n_seq, -1))
    kv_all = jnp.concatenate(behind + ahead[1:], axis=0)
    key_rows = first_row - REACH * rows_here + jnp.arange(block_count * rows_here, dtype=jnp.int32)
    key_layout = layout_rows(key_rows, offsets, grids, row_count)
    attended_output = attend_all(
        query_matrix, kv_all[:, 0], kv_all[:, 1], segment, inside, key_layout[0], key_layout[1]
    )
    attended_flat = attended_output.reshape(rows_here, -1)
    proj_mine = jnp.einsum(
        "tk,jkd->tjd", attended_flat, wo_mine, preferred_element_type=jnp.float32
    ).astype(jnp.bfloat16)
    proj_other = jnp.einsum(
        "tk,jkd->tjd", attended_flat, wo_other, preferred_element_type=jnp.float32
    ).astype(jnp.bfloat16)
    first_half = jnp.where(c == 0, proj_mine, proj_other)
    second_half = jnp.where(c == 0, proj_other, proj_mine)
    share = jnp.stack([first_half, second_half], axis=2).reshape(rows_here, n_zh, n_x, -1)

    by_target = jnp.transpose(share, (2, 0, 1, 3))
    from_peers = lax.all_to_all(by_target, "x", 0, 0, tiled=True)
    total = jnp.sum(from_peers.astype(jnp.float32), axis=0)
    keep = lax.dynamic_index_in_dim(total, zh, axis=1, keepdims=False)
    give = lax.dynamic_index_in_dim(total, 1 - zh, axis=1, keepdims=False)
    head_share = keep + ring(give.astype(jnp.bfloat16), "zh", n_zh, 1).astype(jnp.float32)

    layer_out = (tokens.astype(jnp.float32) + layer_scale * head_share).astype(jnp.bfloat16)
    next_rows = chain(layer_out[:HALO], SEQ, n_seq, -1)
    extended = jnp.concatenate([layer_out, next_rows], axis=0)
    is_corner = is_patch & (grid_row % 2 == 0) & (grid_col % 2 == 0)
    local_ids = jnp.arange(rows_here, dtype=jnp.int32)
    corner_index = jnp.stack(
        [local_ids, local_ids + 1, local_ids + grid_side, local_ids + grid_side + 1], axis=1
    )
    corner_index = jnp.clip(corner_index, 0, extended.shape[0] - 1)
    merged = jnp.take(extended, corner_index, axis=0)
    return jnp.where(is_corner[:, None, None], merged, jnp.zeros_like(merged))


def solution(mesh):
    n_seq, n_tp = mesh.devices.shape
    n_c = 2
    n_y = 4
    n_zh = 2
    sizes = (n_y, n_seq // (n_y * n_c), n_c, n_zh, n_tp // n_zh)
    split = Mesh(mesh.devices.reshape(sizes), ("y", "zl", "c", "zh", "x"))
    placed = (
        P(SEQ, TP),
        P(),
        P(),
        P(SEQ, TP, None, None),
        P(TP, None, SEQ),
        P(TP),
        P(),
        P(),
    )
    return jax.shard_map(
        functools.partial(body, sizes),
        mesh=split,
        in_specs=placed,
        out_specs=P(SEQ, None, TP),
        check_vma=False,
    )
```

```python
import functools
import math

import jax
import jax.numpy as jnp
from jax import lax
from jax.sharding import Mesh, PartitionSpec as P

HALO = 48
REACH = 7


def from_behind(shard, axis, by):
    count = lax.axis_size(axis)
    pairs = [(i, i + by) for i in range(count) if 0 <= i + by < count]
    return lax.ppermute(shard, axis, pairs)


def layout_rows(row_ids, offsets, grids, row_count):
    images = grids.shape[0]
    image_ends = offsets[1:]
    segment = jnp.sum((row_ids[:, None] >= image_ends[None, :]).astype(jnp.int32), axis=1)
    inside = (row_ids >= 0) & (row_ids < row_count) & (segment < images)
    onehot = (
        jnp.minimum(segment, images - 1)[:, None] == jnp.arange(images, dtype=jnp.int32)[None, :]
    ).astype(jnp.int32)
    image_start = jnp.sum(onehot * offsets[None, :-1], axis=1)
    grid_side = jnp.sum(onehot * grids[None, :], axis=1)
    position = row_ids - image_start
    is_patch = inside & (position >= 5)
    patch_index = jnp.maximum(position - 5, 0)
    return (segment, inside, is_patch, patch_index // grid_side, patch_index % grid_side, grid_side)


def rotate(vectors, is_patch, grid_row, grid_col, grid_side):
    quarter = vectors.shape[-1] // 4
    frequency = 2.0 * math.pi * jnp.power(100.0, -jnp.arange(quarter, dtype=jnp.float32) / quarter)
    side_float = grid_side.astype(jnp.float32)
    coord_row = (2 * grid_row + 1).astype(jnp.float32) / side_float - 1.0
    coord_col = (2 * grid_col + 1).astype(jnp.float32) / side_float - 1.0
    angles_row = jnp.where(is_patch[:, None], coord_row[:, None] * frequency[None, :], 0.0)
    angles_col = jnp.where(is_patch[:, None], coord_col[:, None] * frequency[None, :], 0.0)

    def rotate_half(block_vals, angles):
        first_half = block_vals[..., :quarter]
        second_half = block_vals[..., quarter:]
        cosine = jnp.cos(angles)[:, None, :]
        sine_part = jnp.sin(angles)[:, None, :]
        return jnp.concatenate(
            [
                first_half * cosine - second_half * sine_part,
                second_half * cosine + first_half * sine_part,
            ],
            axis=-1,
        )

    return jnp.concatenate(
        [
            rotate_half(vectors[..., : 2 * quarter], angles_row),
            rotate_half(vectors[..., 2 * quarter :], angles_col),
        ],
        axis=-1,
    )


def attend_all(query_matrix, block_of_keys, block_of_values, query_segment, query_inside, key_segment, key_inside):
    logit_scale_factor = 1.0 / math.sqrt(query_matrix.shape[-1])
    attention_logits = (
        jnp.einsum("ecn,dcn->ced", query_matrix, block_of_keys, preferred_element_type=jnp.float32)
        * logit_scale_factor
    )
    allowed = (
        query_inside[:, None]
        & key_inside[None, :]
        & (query_segment[:, None] == key_segment[None, :])
    )
    masked = jnp.where(allowed[None], attention_logits, -1e30)
    row_max = jnp.max(masked, axis=2, keepdims=True)
    exp_terms = jnp.where(allowed[None], jnp.exp(masked - row_max), 0.0)
    row_total = jnp.sum(exp_terms, axis=2, keepdims=True)
    row_total = jnp.where(query_inside[None, :, None], row_total, 1.0)
    softmax_probabilities = (exp_terms / row_total).astype(jnp.bfloat16)
    attended_output = jnp.einsum(
        "vgm,mvb->gvb", softmax_probabilities, block_of_values, preferred_element_type=jnp.float32
    )
    attended_output = jnp.where(query_inside[:, None, None], attended_output, 0.0)
    return attended_output.astype(jnp.bfloat16)


SEQ = ("y", "zl", "c")
TP = ("zh", "x")


def ring(shard, axis, size, by):
    return lax.ppermute(shard, axis, [(i, (i + by) % size) for i in range(size)])


def chain(shard, axis, size, by):
    pairs = [(i, i + by) for i in range(size) if 0 <= i + by < size]
    return lax.ppermute(shard, axis, pairs)


def everyone(block, axis, size):
    repeated = jnp.broadcast_to(block[None], (size, *block.shape))
    return lax.all_to_all(repeated, axis, 0, 0, tiled=True)


def gather_seq_blocks(local, n_y, n_zl):
    line = everyone(local, "zl", n_zl)
    return everyone(line, "y", n_y).reshape(n_y * n_zl, *local.shape)


def body(sizes, tokens, ln_gain, ln_bias, w_qkv, w_out, layer_scale, grids, offsets):
    n_y, n_zl, n_c, n_zh, n_x = sizes
    n_seq = n_y * n_zl * n_c
    rows_here = tokens.shape[0]
    row_count = rows_here * n_seq
    c = lax.axis_index("c")
    zh = lax.axis_index("zh")
    x = lax.axis_index("x")
    seq_index = (lax.axis_index("y") * n_zl + lax.axis_index("zl")) * n_c + c
    first_row = seq_index * rows_here

    wq_local = w_qkv.reshape(w_qkv.shape[0], -1)
    width = wq_local.shape[1]
    wo_rows = -(-w_out.size // (8 * width)) * 8
    wo_padded = jnp.pad(w_out.reshape(-1), (0, wo_rows * width - w_out.size))
    both = jnp.concatenate([wq_local, wo_padded.reshape(wo_rows, width)], axis=0)
    both_mine = gather_seq_blocks(both, n_y, n_zl)
    both_other = ring(both_mine, "c", n_c, 1)
    n_j = n_y * n_zl
    wo_shape = (n_j, w_out.shape[0] * w_out.shape[1], w_out.shape[2])

    def unpack(gathered):
        wq = gathered[:, : wq_local.shape[0]]
        wo = gathered[:, wq_local.shape[0] :].reshape(n_j, -1)[:, : w_out.size].reshape(wo_shape)
        return wq, wo

    wq_mine, wo_mine = unpack(both_mine)
    wq_other, wo_other = unpack(both_other)

    partner = ring(tokens, "zh", n_zh, 1)
    pair = jnp.stack([tokens, partner])
    by_x = everyone(pair, "x", n_x).reshape(n_x, *pair.shape)
    by_zh = jnp.where(zh == 0, by_x, by_x[:, ::-1])
    gathered = jnp.transpose(by_zh, (2, 1, 0, 3)).reshape(rows_here, -1)

    widened = gathered.astype(jnp.float32)
    average = jnp.mean(widened, axis=-1, keepdims=True)
    spread_sq = jnp.mean(jnp.square(widened - average), axis=-1, keepdims=True)
    normed = ((widened - average) * lax.rsqrt(spread_sq + 1e-06) * ln_gain + ln_bias).astype(
        jnp.bfloat16
    )
    normed_v = normed.reshape(rows_here, n_y * n_zl, n_c, -1)
    normed_mine = lax.dynamic_index_in_dim(normed_v, c, axis=2, keepdims=False)
    normed_other = lax.dynamic_index_in_dim(normed_v, 1 - c, axis=2, keepdims=False)
    qkv_sums = (
        jnp.einsum("tjd,jdo->to", normed_mine, wq_mine, preferred_element_type=jnp.float32)
        + jnp.einsum("tjd,jdo->to", normed_other, wq_other, preferred_element_type=jnp.float32)
    ).reshape(rows_here, *w_qkv.shape[1:])
    row_ids = first_row + jnp.arange(rows_here, dtype=jnp.int32)
    segment, inside, is_patch, grid_row, grid_col, grid_side = layout_rows(
        row_ids, offsets, grids, row_count
    )
    query_matrix = rotate(qkv_sums[:, :, 0], is_patch, grid_row, grid_col, grid_side).astype(
        jnp.bfloat16
    )
    roped_keys = rotate(qkv_sums[:, :, 1], is_patch, grid_row, grid_col, grid_side).astype(
        jnp.bfloat16
    )
    values = qkv_sums[:, :, 2].astype(jnp.bfloat16)
    key_value = jnp.stack([roped_keys, values], axis=1)
    block_count = 2 * REACH + 1
    behind = [key_value]
    ahead = [key_value]
    for _ in range(REACH):
        behind.insert(0, chain(behind[0], SEQ, n_seq, 1))
        ahead.append(chain(ahead[-1], SEQ, n_seq, -1))
    kv_all = jnp.concatenate(behind + ahead[1:], axis=0)
    key_rows = first_row - REACH * rows_here + jnp.arange(block_count * rows_here, dtype=jnp.int32)
    key_layout = layout_rows(key_rows, offsets, grids, row_count)
    attended_output = attend_all(
        query_matrix, kv_all[:, 0], kv_all[:, 1], segment, inside, key_layout[0], key_layout[1]
    )
    attended_flat = attended_output.reshape(rows_here, -1)
    proj_mine = jnp.einsum(
        "tk,jkd->tjd", attended_flat, wo_mine, preferred_element_type=jnp.float32
    ).astype(jnp.bfloat16)
    proj_other = jnp.einsum(
        "tk,jkd->tjd", attended_flat, wo_other, preferred_element_type=jnp.float32
    ).astype(jnp.bfloat16)
    first_half = jnp.where(c == 0, proj_mine, proj_other)
    second_half = jnp.where(c == 0, proj_other, proj_mine)
    share = jnp.stack([first_half, second_half], axis=2).reshape(rows_here, n_zh, n_x, -1)

    by_target = jnp.transpose(share, (2, 0, 1, 3))
    from_peers = lax.all_to_all(by_target, "x", 0, 0, tiled=True)
    total = jnp.sum(from_peers.astype(jnp.float32), axis=0)
    keep = lax.dynamic_index_in_dim(total, zh, axis=1, keepdims=False)
    give = lax.dynamic_index_in_dim(total, 1 - zh, axis=1, keepdims=False)
    head_share = keep + ring(give.astype(jnp.bfloat16), "zh", n_zh, 1).astype(jnp.float32)

    layer_out = (tokens.astype(jnp.float32) + layer_scale * head_share).astype(jnp.bfloat16)
    next_rows = chain(layer_out[:HALO], SEQ, n_seq, -1)
    extended = jnp.concatenate([layer_out, next_rows], axis=0)
    is_corner = is_patch & (grid_row % 2 == 0) & (grid_col % 2 == 0)
    local_ids = jnp.arange(rows_here, dtype=jnp.int32)
    corner_index = jnp.stack(
        [local_ids, local_ids + 1, local_ids + grid_side, local_ids + grid_side + 1], axis=1
    )
    corner_index = jnp.clip(corner_index, 0, extended.shape[0] - 1)
    merged = jnp.take(extended, corner_index, axis=0)
    return jnp.where(is_corner[:, None, None], merged, jnp.zeros_like(merged))


def solution(mesh):
    n_seq, n_tp = mesh.devices.shape
    n_c = 2
    n_y = 4
    n_zh = 2
    sizes = (n_y, n_seq // (n_y * n_c), n_c, n_zh, n_tp // n_zh)
    split = Mesh(mesh.devices.reshape(sizes), ("y", "zl", "c", "zh", "x"))
    placed = (
        P(SEQ, TP),
        P(),
        P(),
        P(SEQ, TP, None, None),
        P(TP, None, SEQ),
        P(TP),
        P(),
        P(),
    )
    return jax.shard_map(
        functools.partial(body, sizes),
        mesh=split,
        in_specs=placed,
        out_specs=P(SEQ, None, TP),
        check_vma=False,
    )
```

```python
import functools
import math

import jax
import jax.numpy as jnp
from jax import lax
from jax.sharding import Mesh, PartitionSpec as P

HALO = 48
REACH = 7


def from_behind(shard, axis, by):
    count = lax.axis_size(axis)
    pairs = [(i, i + by) for i in range(count) if 0 <= i + by < count]
    return lax.ppermute(shard, axis, pairs)


def layout_rows(row_ids, offsets, grids, row_count):
    images = grids.shape[0]
    image_ends = offsets[1:]
    segment = jnp.sum((row_ids[:, None] >= image_ends[None, :]).astype(jnp.int32), axis=1)
    inside = (row_ids >= 0) & (row_ids < row_count) & (segment < images)
    onehot = (
        jnp.minimum(segment, images - 1)[:, None] == jnp.arange(images, dtype=jnp.int32)[None, :]
    ).astype(jnp.int32)
    image_start = jnp.sum(onehot * offsets[None, :-1], axis=1)
    grid_side = jnp.sum(onehot * grids[None, :], axis=1)
    position = row_ids - image_start
    is_patch = inside & (position >= 5)
    patch_index = jnp.maximum(position - 5, 0)
    return (segment, inside, is_patch, patch_index // grid_side, patch_index % grid_side, grid_side)


def rotate(vectors, is_patch, grid_row, grid_col, grid_side):
    quarter = vectors.shape[-1] // 4
    frequency = 2.0 * math.pi * jnp.power(100.0, -jnp.arange(quarter, dtype=jnp.float32) / quarter)
    side_float = grid_side.astype(jnp.float32)
    coord_row = (2 * grid_row + 1).astype(jnp.float32) / side_float - 1.0
    coord_col = (2 * grid_col + 1).astype(jnp.float32) / side_float - 1.0
    angles_row = jnp.where(is_patch[:, None], coord_row[:, None] * frequency[None, :], 0.0)
    angles_col = jnp.where(is_patch[:, None], coord_col[:, None] * frequency[None, :], 0.0)

    def rotate_half(block_vals, angles):
        first_half = block_vals[..., :quarter]
        second_half = block_vals[..., quarter:]
        cosine = jnp.cos(angles)[:, None, :]
        sine_part = jnp.sin(angles)[:, None, :]
        return jnp.concatenate(
            [
                first_half * cosine - second_half * sine_part,
                second_half * cosine + first_half * sine_part,
            ],
            axis=-1,
        )

    return jnp.concatenate(
        [
            rotate_half(vectors[..., : 2 * quarter], angles_row),
            rotate_half(vectors[..., 2 * quarter :], angles_col),
        ],
        axis=-1,
    )


def attend_all(query_matrix, block_of_keys, block_of_values, query_segment, query_inside, key_segment, key_inside):
    logit_scale_factor = 1.0 / math.sqrt(query_matrix.shape[-1])
    attention_logits = (
        jnp.einsum("ecn,dcn->ced", query_matrix, block_of_keys, preferred_element_type=jnp.float32)
        * logit_scale_factor
    )
    allowed = (
        query_inside[:, None]
        & key_inside[None, :]
        & (query_segment[:, None] == key_segment[None, :])
    )
    masked = jnp.where(allowed[None], attention_logits, -1e30)
    row_max = jnp.max(masked, axis=2, keepdims=True)
    exp_terms = jnp.where(allowed[None], jnp.exp(masked - row_max), 0.0)
    row_total = jnp.sum(exp_terms, axis=2, keepdims=True)
    row_total = jnp.where(query_inside[None, :, None], row_total, 1.0)
    softmax_probabilities = (exp_terms / row_total).astype(jnp.bfloat16)
    attended_output = jnp.einsum(
        "vgm,mvb->gvb", softmax_probabilities, block_of_values, preferred_element_type=jnp.float32
    )
    attended_output = jnp.where(query_inside[:, None, None], attended_output, 0.0)
    return attended_output.astype(jnp.bfloat16)


SEQ = ("y", "zl", "c")
TP = ("zh", "x")


def ring(shard, axis, size, by):
    return lax.ppermute(shard, axis, [(i, (i + by) % size) for i in range(size)])


def chain(shard, axis, size, by):
    pairs = [(i, i + by) for i in range(size) if 0 <= i + by < size]
    return lax.ppermute(shard, axis, pairs)


def everyone(block, axis, size):
    repeated = jnp.broadcast_to(block[None], (size, *block.shape))
    return lax.all_to_all(repeated, axis, 0, 0, tiled=True)


def gather_seq_blocks(local, n_y, n_zl):
    line = everyone(local, "zl", n_zl)
    return everyone(line, "y", n_y).reshape(n_y * n_zl, *local.shape)


def body(sizes, tokens, ln_gain, ln_bias, w_qkv, w_out, layer_scale, grids, offsets):
    n_y, n_zl, n_c, n_zh, n_x = sizes
    n_seq = n_y * n_zl * n_c
    rows_here = tokens.shape[0]
    row_count = rows_here * n_seq
    c = lax.axis_index("c")
    zh = lax.axis_index("zh")
    x = lax.axis_index("x")
    seq_index = (lax.axis_index("y") * n_zl + lax.axis_index("zl")) * n_c + c
    first_row = seq_index * rows_here

    wq_local = w_qkv.reshape(w_qkv.shape[0], -1)
    wq_mine = gather_seq_blocks(wq_local, n_y, n_zl)
    wq_other = ring(wq_mine, "c", n_c, 1)
    wo_full = lax.all_gather(w_out, SEQ, axis=2, tiled=True)

    partner = ring(tokens, "zh", n_zh, 1)
    pair = jnp.stack([tokens, partner])
    by_x = everyone(pair, "x", n_x).reshape(n_x, *pair.shape)
    by_zh = jnp.where(zh == 0, by_x, by_x[:, ::-1])
    gathered = jnp.transpose(by_zh, (2, 1, 0, 3)).reshape(rows_here, -1)

    widened = gathered.astype(jnp.float32)
    average = jnp.mean(widened, axis=-1, keepdims=True)
    spread_sq = jnp.mean(jnp.square(widened - average), axis=-1, keepdims=True)
    normed = ((widened - average) * lax.rsqrt(spread_sq + 1e-06) * ln_gain + ln_bias).astype(
        jnp.bfloat16
    )
    normed_v = normed.reshape(rows_here, n_y * n_zl, n_c, -1)
    normed_mine = lax.dynamic_index_in_dim(normed_v, c, axis=2, keepdims=False)
    normed_other = lax.dynamic_index_in_dim(normed_v, 1 - c, axis=2, keepdims=False)
    qkv_sums = (
        jnp.einsum("tjd,jdo->to", normed_mine, wq_mine, preferred_element_type=jnp.float32)
        + jnp.einsum("tjd,jdo->to", normed_other, wq_other, preferred_element_type=jnp.float32)
    ).reshape(rows_here, *w_qkv.shape[1:])
    row_ids = first_row + jnp.arange(rows_here, dtype=jnp.int32)
    segment, inside, is_patch, grid_row, grid_col, grid_side = layout_rows(
        row_ids, offsets, grids, row_count
    )
    query_matrix = rotate(qkv_sums[:, :, 0], is_patch, grid_row, grid_col, grid_side).astype(
        jnp.bfloat16
    )
    roped_keys = rotate(qkv_sums[:, :, 1], is_patch, grid_row, grid_col, grid_side).astype(
        jnp.bfloat16
    )
    values = qkv_sums[:, :, 2].astype(jnp.bfloat16)
    key_value = jnp.stack([roped_keys, values], axis=1)
    block_count = 2 * REACH + 1
    behind = [key_value]
    ahead = [key_value]
    for _ in range(REACH):
        behind.insert(0, chain(behind[0], SEQ, n_seq, 1))
        ahead.append(chain(ahead[-1], SEQ, n_seq, -1))
    kv_all = jnp.concatenate(behind + ahead[1:], axis=0)
    key_rows = first_row - REACH * rows_here + jnp.arange(block_count * rows_here, dtype=jnp.int32)
    key_layout = layout_rows(key_rows, offsets, grids, row_count)
    attended_output = attend_all(
        query_matrix, kv_all[:, 0], kv_all[:, 1], segment, inside, key_layout[0], key_layout[1]
    )
    share = jnp.einsum(
        "thf,hfd->td", attended_output, wo_full, preferred_element_type=jnp.float32
    ).astype(jnp.bfloat16).reshape(rows_here, n_zh, n_x, -1)

    by_target = jnp.transpose(share, (2, 0, 1, 3))
    from_peers = lax.all_to_all(by_target, "x", 0, 0, tiled=True)
    total = jnp.sum(from_peers.astype(jnp.float32), axis=0)
    keep = lax.dynamic_index_in_dim(total, zh, axis=1, keepdims=False)
    give = lax.dynamic_index_in_dim(total, 1 - zh, axis=1, keepdims=False)
    head_share = keep + ring(give.astype(jnp.bfloat16), "zh", n_zh, 1).astype(jnp.float32)

    layer_out = (tokens.astype(jnp.float32) + layer_scale * head_share).astype(jnp.bfloat16)
    next_rows = chain(layer_out[:HALO], SEQ, n_seq, -1)
    extended = jnp.concatenate([layer_out, next_rows], axis=0)
    is_corner = is_patch & (grid_row % 2 == 0) & (grid_col % 2 == 0)
    local_ids = jnp.arange(rows_here, dtype=jnp.int32)
    corner_index = jnp.stack(
        [local_ids, local_ids + 1, local_ids + grid_side, local_ids + grid_side + 1], axis=1
    )
    corner_index = jnp.clip(corner_index, 0, extended.shape[0] - 1)
    merged = jnp.take(extended, corner_index, axis=0)
    return jnp.where(is_corner[:, None, None], merged, jnp.zeros_like(merged))


def solution(mesh):
    n_seq, n_tp = mesh.devices.shape
    n_c = 2
    n_y = 4
    n_zh = 2
    sizes = (n_y, n_seq // (n_y * n_c), n_c, n_zh, n_tp // n_zh)
    split = Mesh(mesh.devices.reshape(sizes), ("y", "zl", "c", "zh", "x"))
    placed = (
        P(SEQ, TP),
        P(),
        P(),
        P(SEQ, TP, None, None),
        P(TP, None, SEQ),
        P(TP),
        P(),
        P(),
    )
    return jax.shard_map(
        functools.partial(body, sizes),
        mesh=split,
        in_specs=placed,
        out_specs=P(SEQ, None, TP),
        check_vma=False,
    )
```

```python
import functools
import math

import jax
import jax.numpy as jnp
from jax import lax
from jax.sharding import Mesh, PartitionSpec as P

HALO = 48
REACH = 7


def from_behind(shard, axis, by):
    count = lax.axis_size(axis)
    pairs = [(i, i + by) for i in range(count) if 0 <= i + by < count]
    return lax.ppermute(shard, axis, pairs)


def layout_rows(row_ids, offsets, grids, row_count):
    images = grids.shape[0]
    image_ends = offsets[1:]
    segment = jnp.sum((row_ids[:, None] >= image_ends[None, :]).astype(jnp.int32), axis=1)
    inside = (row_ids >= 0) & (row_ids < row_count) & (segment < images)
    onehot = (
        jnp.minimum(segment, images - 1)[:, None] == jnp.arange(images, dtype=jnp.int32)[None, :]
    ).astype(jnp.int32)
    image_start = jnp.sum(onehot * offsets[None, :-1], axis=1)
    grid_side = jnp.sum(onehot * grids[None, :], axis=1)
    position = row_ids - image_start
    is_patch = inside & (position >= 5)
    patch_index = jnp.maximum(position - 5, 0)
    return (segment, inside, is_patch, patch_index // grid_side, patch_index % grid_side, grid_side)


def rotate(vectors, is_patch, grid_row, grid_col, grid_side):
    quarter = vectors.shape[-1] // 4
    frequency = 2.0 * math.pi * jnp.power(100.0, -jnp.arange(quarter, dtype=jnp.float32) / quarter)
    side_float = grid_side.astype(jnp.float32)
    coord_row = (2 * grid_row + 1).astype(jnp.float32) / side_float - 1.0
    coord_col = (2 * grid_col + 1).astype(jnp.float32) / side_float - 1.0
    angles_row = jnp.where(is_patch[:, None], coord_row[:, None] * frequency[None, :], 0.0)
    angles_col = jnp.where(is_patch[:, None], coord_col[:, None] * frequency[None, :], 0.0)

    def rotate_half(block_vals, angles):
        first_half = block_vals[..., :quarter]
        second_half = block_vals[..., quarter:]
        cosine = jnp.cos(angles)[:, None, :]
        sine_part = jnp.sin(angles)[:, None, :]
        return jnp.concatenate(
            [
                first_half * cosine - second_half * sine_part,
                second_half * cosine + first_half * sine_part,
            ],
            axis=-1,
        )

    return jnp.concatenate(
        [
            rotate_half(vectors[..., : 2 * quarter], angles_row),
            rotate_half(vectors[..., 2 * quarter :], angles_col),
        ],
        axis=-1,
    )


def attend_all(query_matrix, block_of_keys, block_of_values, query_segment, query_inside, key_segment, key_inside):
    logit_scale_factor = 1.0 / math.sqrt(query_matrix.shape[-1])
    attention_logits = (
        jnp.einsum("ecn,dcn->ced", query_matrix, block_of_keys, preferred_element_type=jnp.float32)
        * logit_scale_factor
    )
    allowed = (
        query_inside[:, None]
        & key_inside[None, :]
        & (query_segment[:, None] == key_segment[None, :])
    )
    masked = jnp.where(allowed[None], attention_logits, -1e30)
    row_max = jnp.max(masked, axis=2, keepdims=True)
    exp_terms = jnp.where(allowed[None], jnp.exp(masked - row_max), 0.0)
    row_total = jnp.sum(exp_terms, axis=2, keepdims=True)
    row_total = jnp.where(query_inside[None, :, None], row_total, 1.0)
    softmax_probabilities = (exp_terms / row_total).astype(jnp.bfloat16)
    attended_output = jnp.einsum(
        "vgm,mvb->gvb", softmax_probabilities, block_of_values, preferred_element_type=jnp.float32
    )
    attended_output = jnp.where(query_inside[:, None, None], attended_output, 0.0)
    return attended_output.astype(jnp.bfloat16)


SEQ = ("y", "zl", "c")
TP = ("zh", "x")


def ring(shard, axis, size, by):
    return lax.ppermute(shard, axis, [(i, (i + by) % size) for i in range(size)])


def chain(shard, axis, size, by):
    pairs = [(i, i + by) for i in range(size) if 0 <= i + by < size]
    return lax.ppermute(shard, axis, pairs)


def everyone(block, axis, size):
    repeated = jnp.broadcast_to(block[None], (size, *block.shape))
    return lax.all_to_all(repeated, axis, 0, 0, tiled=True)


def gather_seq_blocks(local, n_y, n_zl):
    line = everyone(local, "zl", n_zl)
    return everyone(line, "y", n_y).reshape(n_y * n_zl, *local.shape)


def body(sizes, tokens, ln_gain, ln_bias, w_qkv, w_out, layer_scale, grids, offsets):
    n_y, n_zl, n_c, n_zh, n_x = sizes
    n_seq = n_y * n_zl * n_c
    rows_here = tokens.shape[0]
    row_count = rows_here * n_seq
    c = lax.axis_index("c")
    zh = lax.axis_index("zh")
    x = lax.axis_index("x")
    seq_index = (lax.axis_index("y") * n_zl + lax.axis_index("zl")) * n_c + c
    first_row = seq_index * rows_here

    wq_local = w_qkv.reshape(w_qkv.shape[0], -1)
    wq_mine = gather_seq_blocks(wq_local, n_y, n_zl)
    wq_other = ring(wq_mine, "c", n_c, 1)
    wo_full = lax.all_gather(w_out, SEQ, axis=2, tiled=True)

    partner = ring(tokens, "zh", n_zh, 1)
    pair = jnp.stack([tokens, partner])
    by_x = everyone(pair, "x", n_x).reshape(n_x, *pair.shape)
    by_zh = jnp.where(zh == 0, by_x, by_x[:, ::-1])
    gathered = jnp.transpose(by_zh, (2, 1, 0, 3)).reshape(rows_here, -1)

    widened = gathered.astype(jnp.float32)
    average = jnp.mean(widened, axis=-1, keepdims=True)
    spread_sq = jnp.mean(jnp.square(widened - average), axis=-1, keepdims=True)
    normed = ((widened - average) * lax.rsqrt(spread_sq + 1e-06) * ln_gain + ln_bias).astype(
        jnp.bfloat16
    )
    normed_v = normed.reshape(rows_here, n_y * n_zl, n_c, -1)
    normed_mine = lax.dynamic_index_in_dim(normed_v, c, axis=2, keepdims=False)
    normed_other = lax.dynamic_index_in_dim(normed_v, 1 - c, axis=2, keepdims=False)
    qkv_sums = (
        jnp.einsum("tjd,jdo->to", normed_mine, wq_mine, preferred_element_type=jnp.float32)
        + jnp.einsum("tjd,jdo->to", normed_other, wq_other, preferred_element_type=jnp.float32)
    ).reshape(rows_here, *w_qkv.shape[1:])
    row_ids = first_row + jnp.arange(rows_here, dtype=jnp.int32)
    segment, inside, is_patch, grid_row, grid_col, grid_side = layout_rows(
        row_ids, offsets, grids, row_count
    )
    query_matrix = rotate(qkv_sums[:, :, 0], is_patch, grid_row, grid_col, grid_side).astype(
        jnp.bfloat16
    )
    roped_keys = rotate(qkv_sums[:, :, 1], is_patch, grid_row, grid_col, grid_side).astype(
        jnp.bfloat16
    )
    values = qkv_sums[:, :, 2].astype(jnp.bfloat16)
    key_value = jnp.stack([roped_keys, values], axis=1)
    block_count = 2 * REACH + 1
    near = {0: key_value}
    for sign in (1, -1):
        odd = chain(key_value, SEQ, n_seq, sign)
        even = chain(key_value, SEQ, n_seq, 2 * sign)
        near[sign], near[2 * sign] = odd, even
        for distance in range(3, REACH + 1):
            if distance % 2:
                odd = chain(odd, SEQ, n_seq, 2 * sign)
                near[distance * sign] = odd
            else:
                even = chain(even, SEQ, n_seq, 2 * sign)
                near[distance * sign] = even
    kv_all = jnp.concatenate([near[d] for d in range(-REACH, REACH + 1)][::-1], axis=0)
    key_rows = first_row - REACH * rows_here + jnp.arange(block_count * rows_here, dtype=jnp.int32)
    key_layout = layout_rows(key_rows, offsets, grids, row_count)
    attended_output = attend_all(
        query_matrix, kv_all[:, 0], kv_all[:, 1], segment, inside, key_layout[0], key_layout[1]
    )
    share = jnp.einsum(
        "thf,hfd->td", attended_output, wo_full, preferred_element_type=jnp.float32
    ).astype(jnp.bfloat16).reshape(rows_here, n_zh, n_x, -1)

    by_target = jnp.transpose(share, (2, 0, 1, 3))
    from_peers = lax.all_to_all(by_target, "x", 0, 0, tiled=True)
    total = jnp.sum(from_peers.astype(jnp.float32), axis=0)
    keep = lax.dynamic_index_in_dim(total, zh, axis=1, keepdims=False)
    give = lax.dynamic_index_in_dim(total, 1 - zh, axis=1, keepdims=False)
    head_share = keep + ring(give.astype(jnp.bfloat16), "zh", n_zh, 1).astype(jnp.float32)

    layer_out = (tokens.astype(jnp.float32) + layer_scale * head_share).astype(jnp.bfloat16)
    next_rows = chain(layer_out[:HALO], SEQ, n_seq, -1)
    extended = jnp.concatenate([layer_out, next_rows], axis=0)
    is_corner = is_patch & (grid_row % 2 == 0) & (grid_col % 2 == 0)
    local_ids = jnp.arange(rows_here, dtype=jnp.int32)
    corner_index = jnp.stack(
        [local_ids, local_ids + 1, local_ids + grid_side, local_ids + grid_side + 1], axis=1
    )
    corner_index = jnp.clip(corner_index, 0, extended.shape[0] - 1)
    merged = jnp.take(extended, corner_index, axis=0)
    return jnp.where(is_corner[:, None, None], merged, jnp.zeros_like(merged))


def solution(mesh):
    n_seq, n_tp = mesh.devices.shape
    n_c = 2
    n_y = 4
    n_zh = 2
    sizes = (n_y, n_seq // (n_y * n_c), n_c, n_zh, n_tp // n_zh)
    split = Mesh(mesh.devices.reshape(sizes), ("y", "zl", "c", "zh", "x"))
    placed = (
        P(SEQ, TP),
        P(),
        P(),
        P(SEQ, TP, None, None),
        P(TP, None, SEQ),
        P(TP),
        P(),
        P(),
    )
    return jax.shard_map(
        functools.partial(body, sizes),
        mesh=split,
        in_specs=placed,
        out_specs=P(SEQ, None, TP),
        check_vma=False,
    )
```

```python
import functools
import math

import jax
import jax.numpy as jnp
from jax import lax
from jax.sharding import Mesh, PartitionSpec as P

HALO = 48
REACH = 7


def from_behind(shard, axis, by):
    count = lax.axis_size(axis)
    pairs = [(i, i + by) for i in range(count) if 0 <= i + by < count]
    return lax.ppermute(shard, axis, pairs)


def layout_rows(row_ids, offsets, grids, row_count):
    images = grids.shape[0]
    image_ends = offsets[1:]
    segment = jnp.sum((row_ids[:, None] >= image_ends[None, :]).astype(jnp.int32), axis=1)
    inside = (row_ids >= 0) & (row_ids < row_count) & (segment < images)
    onehot = (
        jnp.minimum(segment, images - 1)[:, None] == jnp.arange(images, dtype=jnp.int32)[None, :]
    ).astype(jnp.int32)
    image_start = jnp.sum(onehot * offsets[None, :-1], axis=1)
    grid_side = jnp.sum(onehot * grids[None, :], axis=1)
    position = row_ids - image_start
    is_patch = inside & (position >= 5)
    patch_index = jnp.maximum(position - 5, 0)
    return (segment, inside, is_patch, patch_index // grid_side, patch_index % grid_side, grid_side)


def rotate(vectors, is_patch, grid_row, grid_col, grid_side):
    quarter = vectors.shape[-1] // 4
    frequency = 2.0 * math.pi * jnp.power(100.0, -jnp.arange(quarter, dtype=jnp.float32) / quarter)
    side_float = grid_side.astype(jnp.float32)
    coord_row = (2 * grid_row + 1).astype(jnp.float32) / side_float - 1.0
    coord_col = (2 * grid_col + 1).astype(jnp.float32) / side_float - 1.0
    angles_row = jnp.where(is_patch[:, None], coord_row[:, None] * frequency[None, :], 0.0)
    angles_col = jnp.where(is_patch[:, None], coord_col[:, None] * frequency[None, :], 0.0)

    def rotate_half(block_vals, angles):
        first_half = block_vals[..., :quarter]
        second_half = block_vals[..., quarter:]
        cosine = jnp.cos(angles)[:, None, :]
        sine_part = jnp.sin(angles)[:, None, :]
        return jnp.concatenate(
            [
                first_half * cosine - second_half * sine_part,
                second_half * cosine + first_half * sine_part,
            ],
            axis=-1,
        )

    return jnp.concatenate(
        [
            rotate_half(vectors[..., : 2 * quarter], angles_row),
            rotate_half(vectors[..., 2 * quarter :], angles_col),
        ],
        axis=-1,
    )


def attend_all(query_matrix, block_of_keys, block_of_values, query_segment, query_inside, key_segment, key_inside):
    logit_scale_factor = 1.0 / math.sqrt(query_matrix.shape[-1])
    attention_logits = (
        jnp.einsum("ecn,dcn->ced", query_matrix, block_of_keys, preferred_element_type=jnp.float32)
        * logit_scale_factor
    )
    allowed = (
        query_inside[:, None]
        & key_inside[None, :]
        & (query_segment[:, None] == key_segment[None, :])
    )
    masked = jnp.where(allowed[None], attention_logits, -1e30)
    row_max = jnp.max(masked, axis=2, keepdims=True)
    exp_terms = jnp.where(allowed[None], jnp.exp(masked - row_max), 0.0)
    row_total = jnp.sum(exp_terms, axis=2, keepdims=True)
    row_total = jnp.where(query_inside[None, :, None], row_total, 1.0)
    softmax_probabilities = (exp_terms / row_total).astype(jnp.bfloat16)
    attended_output = jnp.einsum(
        "vgm,mvb->gvb", softmax_probabilities, block_of_values, preferred_element_type=jnp.float32
    )
    attended_output = jnp.where(query_inside[:, None, None], attended_output, 0.0)
    return attended_output.astype(jnp.bfloat16)


SEQ = ("y", "zl", "c")
TP = ("zh", "x")


def ring(shard, axis, size, by):
    return lax.ppermute(shard, axis, [(i, (i + by) % size) for i in range(size)])


def chain(shard, axis, size, by):
    pairs = [(i, i + by) for i in range(size) if 0 <= i + by < size]
    return lax.ppermute(shard, axis, pairs)


def everyone(block, axis, size):
    repeated = jnp.broadcast_to(block[None], (size, *block.shape))
    return lax.all_to_all(repeated, axis, 0, 0, tiled=True)


def gather_seq_blocks(local, n_y, n_zl):
    line = everyone(local, "zl", n_zl)
    return everyone(line, "y", n_y).reshape(n_y * n_zl, *local.shape)


def body(sizes, tokens, ln_gain, ln_bias, w_qkv, w_out, layer_scale, grids, offsets):
    n_y, n_zl, n_c, n_zh, n_x = sizes
    n_seq = n_y * n_zl * n_c
    rows_here = tokens.shape[0]
    row_count = rows_here * n_seq
    c = lax.axis_index("c")
    zh = lax.axis_index("zh")
    x = lax.axis_index("x")
    seq_index = (lax.axis_index("y") * n_zl + lax.axis_index("zl")) * n_c + c
    first_row = seq_index * rows_here

    wq_local = w_qkv.reshape(w_qkv.shape[0], -1)
    wq_mine = gather_seq_blocks(wq_local, n_y, n_zl)
    wq_other = ring(wq_mine, "c", n_c, 1)
    wo_full = lax.all_gather(w_out, SEQ, axis=2, tiled=True)

    partner = ring(tokens, "zh", n_zh, 1)
    pair = jnp.stack([tokens, partner])
    by_x = everyone(pair, "x", n_x).reshape(n_x, *pair.shape)
    by_zh = jnp.where(zh == 0, by_x, by_x[:, ::-1])
    gathered = jnp.transpose(by_zh, (2, 1, 0, 3)).reshape(rows_here, -1)

    widened = gathered.astype(jnp.float32)
    average = jnp.mean(widened, axis=-1, keepdims=True)
    spread_sq = jnp.mean(jnp.square(widened - average), axis=-1, keepdims=True)
    normed = ((widened - average) * lax.rsqrt(spread_sq + 1e-06) * ln_gain + ln_bias).astype(
        jnp.bfloat16
    )
    normed_v = normed.reshape(rows_here, n_y * n_zl, n_c, -1)
    normed_mine = lax.dynamic_index_in_dim(normed_v, c, axis=2, keepdims=False)
    normed_other = lax.dynamic_index_in_dim(normed_v, 1 - c, axis=2, keepdims=False)
    qkv_sums = (
        jnp.einsum("tjd,jdo->to", normed_mine, wq_mine, preferred_element_type=jnp.float32)
        + jnp.einsum("tjd,jdo->to", normed_other, wq_other, preferred_element_type=jnp.float32)
    ).reshape(rows_here, *w_qkv.shape[1:])
    row_ids = first_row + jnp.arange(rows_here, dtype=jnp.int32)
    segment, inside, is_patch, grid_row, grid_col, grid_side = layout_rows(
        row_ids, offsets, grids, row_count
    )
    query_matrix = rotate(qkv_sums[:, :, 0], is_patch, grid_row, grid_col, grid_side).astype(
        jnp.bfloat16
    )
    roped_keys = rotate(qkv_sums[:, :, 1], is_patch, grid_row, grid_col, grid_side).astype(
        jnp.bfloat16
    )
    values = qkv_sums[:, :, 2].astype(jnp.bfloat16)
    key_value = jnp.stack([roped_keys, values], axis=1)
    block_count = 2 * REACH + 1
    near = {0: key_value}
    for sign in (1, -1):
        odd = chain(key_value, SEQ, n_seq, sign)
        even = chain(key_value, SEQ, n_seq, 2 * sign)
        near[sign], near[2 * sign] = odd, even
        for distance in range(3, REACH + 1):
            if distance % 2:
                odd = chain(odd, SEQ, n_seq, 2 * sign)
                near[distance * sign] = odd
            else:
                even = chain(even, SEQ, n_seq, 2 * sign)
                near[distance * sign] = even
    kv_all = jnp.concatenate([near[d] for d in range(-REACH, REACH + 1)][::-1], axis=0)
    key_rows = first_row - REACH * rows_here + jnp.arange(block_count * rows_here, dtype=jnp.int32)
    key_layout = layout_rows(key_rows, offsets, grids, row_count)
    attended_output = attend_all(
        query_matrix, kv_all[:, 0], kv_all[:, 1], segment, inside, key_layout[0], key_layout[1]
    )
    wo_by_target = wo_full.reshape(*wo_full.shape[:2], n_zh, n_x, -1)
    by_target = jnp.einsum(
        "thf,hfzxd->xtzd", attended_output, wo_by_target, preferred_element_type=jnp.float32
    ).astype(jnp.bfloat16)

    from_peers = lax.all_to_all(by_target, "x", 0, 0, tiled=True)
    total = jnp.sum(from_peers.astype(jnp.float32), axis=0)
    keep = lax.dynamic_index_in_dim(total, zh, axis=1, keepdims=False)
    give = lax.dynamic_index_in_dim(total, 1 - zh, axis=1, keepdims=False)
    head_share = keep + ring(give.astype(jnp.bfloat16), "zh", n_zh, 1).astype(jnp.float32)

    layer_out = (tokens.astype(jnp.float32) + layer_scale * head_share).astype(jnp.bfloat16)
    next_rows = chain(layer_out[:HALO], SEQ, n_seq, -1)
    extended = jnp.concatenate([layer_out, next_rows], axis=0)
    is_corner = is_patch & (grid_row % 2 == 0) & (grid_col % 2 == 0)
    local_ids = jnp.arange(rows_here, dtype=jnp.int32)
    corner_index = jnp.stack(
        [local_ids, local_ids + 1, local_ids + grid_side, local_ids + grid_side + 1], axis=1
    )
    corner_index = jnp.clip(corner_index, 0, extended.shape[0] - 1)
    merged = jnp.take(extended, corner_index, axis=0)
    return jnp.where(is_corner[:, None, None], merged, jnp.zeros_like(merged))


def solution(mesh):
    n_seq, n_tp = mesh.devices.shape
    n_c = 2
    n_y = 4
    n_zh = 2
    sizes = (n_y, n_seq // (n_y * n_c), n_c, n_zh, n_tp // n_zh)
    split = Mesh(mesh.devices.reshape(sizes), ("y", "zl", "c", "zh", "x"))
    placed = (
        P(SEQ, TP),
        P(),
        P(),
        P(SEQ, TP, None, None),
        P(TP, None, SEQ),
        P(TP),
        P(),
        P(),
    )
    return jax.shard_map(
        functools.partial(body, sizes),
        mesh=split,
        in_specs=placed,
        out_specs=P(SEQ, None, TP),
        check_vma=False,
    )
```

```python
import functools
import math

import jax
import jax.numpy as jnp
from jax import lax
from jax.sharding import Mesh, PartitionSpec as P


HALO = 48
REACH = 7


def layout_rows(row_ids, offsets, grids, row_count):
    images = grids.shape[0]
    image_ends = offsets[1:]
    segment = jnp.sum((row_ids[:, None] >= image_ends[None, :]).astype(jnp.int32), axis=1)
    inside = (row_ids >= 0) & (row_ids < row_count) & (segment < images)
    onehot = (
        jnp.minimum(segment, images - 1)[:, None] == jnp.arange(images, dtype=jnp.int32)[None, :]
    ).astype(jnp.int32)
    image_start = jnp.sum(onehot * offsets[None, :-1], axis=1)
    grid_side = jnp.sum(onehot * grids[None, :], axis=1)
    position = row_ids - image_start
    is_patch = inside & (position >= 5)
    patch_index = jnp.maximum(position - 5, 0)
    return (segment, inside, is_patch, patch_index // grid_side, patch_index % grid_side, grid_side)


def rotate(vectors, is_patch, grid_row, grid_col, grid_side):
    quarter = vectors.shape[-1] // 4
    frequency = 2.0 * math.pi * jnp.power(100.0, -jnp.arange(quarter, dtype=jnp.float32) / quarter)
    side_float = grid_side.astype(jnp.float32)
    coord_row = (2 * grid_row + 1).astype(jnp.float32) / side_float - 1.0
    coord_col = (2 * grid_col + 1).astype(jnp.float32) / side_float - 1.0
    angles_row = jnp.where(is_patch[:, None], coord_row[:, None] * frequency[None, :], 0.0)
    angles_col = jnp.where(is_patch[:, None], coord_col[:, None] * frequency[None, :], 0.0)

    def rotate_half(block_vals, angles):
        first_half = block_vals[..., :quarter]
        second_half = block_vals[..., quarter:]
        cosine = jnp.cos(angles)[:, None, :]
        sine_part = jnp.sin(angles)[:, None, :]
        return jnp.concatenate(
            [
                first_half * cosine - second_half * sine_part,
                second_half * cosine + first_half * sine_part,
            ],
            axis=-1,
        )

    return jnp.concatenate(
        [
            rotate_half(vectors[..., : 2 * quarter], angles_row),
            rotate_half(vectors[..., 2 * quarter :], angles_col),
        ],
        axis=-1,
    )


def attend_all(query_matrix, block_of_keys, block_of_values, query_segment, query_inside, key_segment, key_inside):
    logit_scale_factor = 1.0 / math.sqrt(query_matrix.shape[-1])
    attention_logits = (
        jnp.einsum("ecn,dcn->ced", query_matrix, block_of_keys, preferred_element_type=jnp.float32)
        * logit_scale_factor
    )
    allowed = (
        query_inside[:, None]
        & key_inside[None, :]
        & (query_segment[:, None] == key_segment[None, :])
    )
    masked = jnp.where(allowed[None], attention_logits, -1e30)
    row_max = jnp.max(masked, axis=2, keepdims=True)
    exp_terms = jnp.where(allowed[None], jnp.exp(masked - row_max), 0.0)
    row_total = jnp.sum(exp_terms, axis=2, keepdims=True)
    row_total = jnp.where(query_inside[None, :, None], row_total, 1.0)
    softmax_probabilities = (exp_terms / row_total).astype(jnp.bfloat16)
    attended_output = jnp.einsum(
        "vgm,mvb->gvb", softmax_probabilities, block_of_values, preferred_element_type=jnp.float32
    )
    attended_output = jnp.where(query_inside[:, None, None], attended_output, 0.0)
    return attended_output.astype(jnp.bfloat16)


SEQ = ("y", "zl", "c")
TP = ("zh", "x")


def ring(shard, axis, size, by):
    return lax.ppermute(shard, axis, [(i, (i + by) % size) for i in range(size)])


def chain(shard, axis, size, by):
    pairs = [(i, i + by) for i in range(size) if 0 <= i + by < size]
    return lax.ppermute(shard, axis, pairs)


def everyone(block, axis, size):
    repeated = jnp.broadcast_to(block[None], (size, *block.shape))
    return lax.all_to_all(repeated, axis, 0, 0, tiled=True)


def gather_seq_blocks(local, n_y, n_zl):
    line = everyone(local, "zl", n_zl)
    return everyone(line, "y", n_y).reshape(n_y * n_zl, *local.shape)


def body(sizes, *args):
    return layer(sizes, *args)


def layer(sizes, tokens, ln_gain, ln_bias, w_qkv, w_out, layer_scale, grids, offsets):
    n_y, n_zl, n_c, n_zh, n_x = sizes
    n_seq = n_y * n_zl * n_c
    rows_here = tokens.shape[0]
    row_count = rows_here * n_seq
    c = lax.axis_index("c")
    zh = lax.axis_index("zh")
    seq_index = (lax.axis_index("y") * n_zl + lax.axis_index("zl")) * n_c + c
    first_row = seq_index * rows_here

    wq_local = w_qkv.reshape(w_qkv.shape[0], -1)
    wq_mine = gather_seq_blocks(wq_local, n_y, n_zl)
    wq_other = ring(wq_mine, "c", n_c, 1)
    wo_full = lax.all_gather(w_out, SEQ, axis=2, tiled=True)

    partner = ring(tokens, "zh", n_zh, 1)
    pair = jnp.stack([tokens, partner])
    by_x = everyone(pair, "x", n_x).reshape(n_x, *pair.shape)
    by_zh = jnp.where(zh == 0, by_x, by_x[:, ::-1])
    gathered = jnp.transpose(by_zh, (2, 1, 0, 3)).reshape(rows_here, -1)

    widened = gathered.astype(jnp.float32)
    average = jnp.mean(widened, axis=-1, keepdims=True)
    spread_sq = jnp.mean(jnp.square(widened - average), axis=-1, keepdims=True)
    normed = ((widened - average) * lax.rsqrt(spread_sq + 1e-06) * ln_gain + ln_bias).astype(
        jnp.bfloat16
    )
    normed_v = normed.reshape(rows_here, n_y * n_zl, n_c, -1)
    normed_mine = lax.dynamic_index_in_dim(normed_v, c, axis=2, keepdims=False)
    normed_other = lax.dynamic_index_in_dim(normed_v, 1 - c, axis=2, keepdims=False)
    qkv_sums = (
        jnp.einsum("tjd,jdo->to", normed_mine, wq_mine, preferred_element_type=jnp.float32)
        + jnp.einsum("tjd,jdo->to", normed_other, wq_other, preferred_element_type=jnp.float32)
    ).reshape(rows_here, *w_qkv.shape[1:])
    row_ids = first_row + jnp.arange(rows_here, dtype=jnp.int32)
    segment, inside, is_patch, grid_row, grid_col, grid_side = layout_rows(
        row_ids, offsets, grids, row_count
    )
    query_matrix = rotate(qkv_sums[:, :, 0], is_patch, grid_row, grid_col, grid_side).astype(
        jnp.bfloat16
    )
    roped_keys = rotate(qkv_sums[:, :, 1], is_patch, grid_row, grid_col, grid_side).astype(
        jnp.bfloat16
    )
    values = qkv_sums[:, :, 2].astype(jnp.bfloat16)
    key_value = jnp.stack([roped_keys, values], axis=1)
    block_count = 2 * REACH + 1
    near = {0: key_value}
    for sign in (1, -1):
        odd = chain(key_value, SEQ, n_seq, sign)
        even = chain(key_value, SEQ, n_seq, 2 * sign)
        near[sign], near[2 * sign] = odd, even
        for distance in range(3, REACH + 1):
            if distance % 2:
                odd = chain(odd, SEQ, n_seq, 2 * sign)
                near[distance * sign] = odd
            else:
                even = chain(even, SEQ, n_seq, 2 * sign)
                near[distance * sign] = even
    kv_all = jnp.concatenate([near[d] for d in range(-REACH, REACH + 1)][::-1], axis=0)
    key_rows = first_row - REACH * rows_here + jnp.arange(block_count * rows_here, dtype=jnp.int32)
    key_layout = layout_rows(key_rows, offsets, grids, row_count)
    attended_output = attend_all(
        query_matrix, kv_all[:, 0], kv_all[:, 1], segment, inside, key_layout[0], key_layout[1]
    )
    wo_by_target = wo_full.reshape(*wo_full.shape[:2], n_zh, n_x, -1)
    by_target = jnp.einsum(
        "thf,hfzxd->xtzd", attended_output, wo_by_target, preferred_element_type=jnp.float32
    ).astype(jnp.bfloat16)

    from_peers = lax.all_to_all(by_target, "x", 0, 0, tiled=True)
    total = jnp.sum(from_peers.astype(jnp.float32), axis=0)
    keep = lax.dynamic_index_in_dim(total, zh, axis=1, keepdims=False)
    give = lax.dynamic_index_in_dim(total, 1 - zh, axis=1, keepdims=False)
    head_share = keep + ring(give.astype(jnp.bfloat16), "zh", n_zh, 1).astype(jnp.float32)

    layer_out = (tokens.astype(jnp.float32) + layer_scale * head_share).astype(jnp.bfloat16)
    next_rows = chain(layer_out[:HALO], SEQ, n_seq, -1)
    extended = jnp.concatenate([layer_out, next_rows], axis=0)
    is_corner = is_patch & (grid_row % 2 == 0) & (grid_col % 2 == 0)
    local_ids = jnp.arange(rows_here, dtype=jnp.int32)
    corner_index = jnp.stack(
        [local_ids, local_ids + 1, local_ids + grid_side, local_ids + grid_side + 1], axis=1
    )
    corner_index = jnp.clip(corner_index, 0, extended.shape[0] - 1)
    merged = jnp.take(extended, corner_index, axis=0)
    return jnp.where(is_corner[:, None, None], merged, jnp.zeros_like(merged))


def solution(mesh):
    n_seq, n_tp = mesh.devices.shape
    n_c = 2
    n_y = 4
    n_zh = 2
    sizes = (n_y, n_seq // (n_y * n_c), n_c, n_zh, n_tp // n_zh)
    split = Mesh(mesh.devices.reshape(sizes), ("y", "zl", "c", "zh", "x"))
    placed = (
        P(SEQ, TP),
        P(),
        P(),
        P(SEQ, TP, None, None),
        P(TP, None, SEQ),
        P(TP),
        P(),
        P(),
    )
    return jax.shard_map(
        functools.partial(body, sizes),
        mesh=split,
        in_specs=placed,
        out_specs=P(SEQ, None, TP),
        check_vma=False,
    )
```

```python
import functools
import math

import jax
import jax.numpy as jnp
from jax import lax
from jax.sharding import Mesh, PartitionSpec as P

HALO = 48
REACH = 7


def from_behind(shard, axis, by):
    count = lax.axis_size(axis)
    pairs = [(i, i + by) for i in range(count) if 0 <= i + by < count]
    return lax.ppermute(shard, axis, pairs)


def layout_rows(row_ids, offsets, grids, row_count):
    images = grids.shape[0]
    image_ends = offsets[1:]
    segment = jnp.sum((row_ids[:, None] >= image_ends[None, :]).astype(jnp.int32), axis=1)
    inside = (row_ids >= 0) & (row_ids < row_count) & (segment < images)
    onehot = (
        jnp.minimum(segment, images - 1)[:, None] == jnp.arange(images, dtype=jnp.int32)[None, :]
    ).astype(jnp.int32)
    image_start = jnp.sum(onehot * offsets[None, :-1], axis=1)
    grid_side = jnp.sum(onehot * grids[None, :], axis=1)
    position = row_ids - image_start
    is_patch = inside & (position >= 5)
    patch_index = jnp.maximum(position - 5, 0)
    return (segment, inside, is_patch, patch_index // grid_side, patch_index % grid_side, grid_side)


def rotate(vectors, is_patch, grid_row, grid_col, grid_side):
    quarter = vectors.shape[-1] // 4
    frequency = 2.0 * math.pi * jnp.power(100.0, -jnp.arange(quarter, dtype=jnp.float32) / quarter)
    side_float = grid_side.astype(jnp.float32)
    coord_row = (2 * grid_row + 1).astype(jnp.float32) / side_float - 1.0
    coord_col = (2 * grid_col + 1).astype(jnp.float32) / side_float - 1.0
    angles_row = jnp.where(is_patch[:, None], coord_row[:, None] * frequency[None, :], 0.0)
    angles_col = jnp.where(is_patch[:, None], coord_col[:, None] * frequency[None, :], 0.0)

    def rotate_half(block_vals, angles):
        first_half = block_vals[..., :quarter]
        second_half = block_vals[..., quarter:]
        cosine = jnp.cos(angles)[:, None, :]
        sine_part = jnp.sin(angles)[:, None, :]
        return jnp.concatenate(
            [
                first_half * cosine - second_half * sine_part,
                second_half * cosine + first_half * sine_part,
            ],
            axis=-1,
        )

    return jnp.concatenate(
        [
            rotate_half(vectors[..., : 2 * quarter], angles_row),
            rotate_half(vectors[..., 2 * quarter :], angles_col),
        ],
        axis=-1,
    )


def attend_all(query_matrix, block_of_keys, block_of_values, query_segment, query_inside, key_segment, key_inside):
    logit_scale_factor = 1.0 / math.sqrt(query_matrix.shape[-1])
    attention_logits = (
        jnp.einsum("ecn,dcn->ced", query_matrix, block_of_keys, preferred_element_type=jnp.float32)
        * logit_scale_factor
    )
    allowed = (
        query_inside[:, None]
        & key_inside[None, :]
        & (query_segment[:, None] == key_segment[None, :])
    )
    masked = jnp.where(allowed[None], attention_logits, -1e30)
    row_max = jnp.max(masked, axis=2, keepdims=True)
    exp_terms = jnp.where(allowed[None], jnp.exp(masked - row_max), 0.0)
    row_total = jnp.sum(exp_terms, axis=2, keepdims=True)
    row_total = jnp.where(query_inside[None, :, None], row_total, 1.0)
    softmax_probabilities = (exp_terms / row_total).astype(jnp.bfloat16)
    attended_output = jnp.einsum(
        "vgm,mvb->gvb", softmax_probabilities, block_of_values, preferred_element_type=jnp.float32
    )
    attended_output = jnp.where(query_inside[:, None, None], attended_output, 0.0)
    return attended_output.astype(jnp.bfloat16)


SEQ = ("y", "zl", "c")
TP = ("zh", "x")


def ring(shard, axis, size, by):
    return lax.ppermute(shard, axis, [(i, (i + by) % size) for i in range(size)])


def chain(shard, axis, size, by):
    pairs = [(i, i + by) for i in range(size) if 0 <= i + by < size]
    return lax.ppermute(shard, axis, pairs)


def everyone(block, axis, size):
    repeated = jnp.broadcast_to(block[None], (size, *block.shape))
    return lax.all_to_all(repeated, axis, 0, 0, tiled=True)


def gather_seq_blocks(local, n_y, n_zl):
    line = everyone(local, "zl", n_zl)
    return everyone(line, "y", n_y).reshape(n_y * n_zl, *local.shape)


def body(sizes, tokens, ln_gain, ln_bias, w_qkv, w_out, layer_scale, grids, offsets):
    n_y, n_zl, n_c, n_zh, n_x = sizes
    n_seq = n_y * n_zl * n_c
    rows_here = tokens.shape[0]
    row_count = rows_here * n_seq
    c = lax.axis_index("c")
    zh = lax.axis_index("zh")
    x = lax.axis_index("x")
    seq_index = (lax.axis_index("y") * n_zl + lax.axis_index("zl")) * n_c + c
    first_row = seq_index * rows_here

    wq_local = w_qkv.reshape(w_qkv.shape[0], -1)
    wq_mine = gather_seq_blocks(wq_local, n_y, n_zl)
    wq_other = ring(wq_mine, "c", n_c, 1)
    wo_full = lax.all_gather(w_out, SEQ, axis=2, tiled=True)

    partner = ring(tokens, "zh", n_zh, 1)
    pair = jnp.where(zh == 0, jnp.stack([tokens, partner]), jnp.stack([partner, tokens]))
    by_zh = everyone(pair, "x", n_x).reshape(n_x, *pair.shape)
    gathered = jnp.transpose(by_zh, (2, 1, 0, 3)).reshape(rows_here, -1)

    widened = gathered.astype(jnp.float32)
    average = jnp.mean(widened, axis=-1, keepdims=True)
    spread_sq = jnp.mean(jnp.square(widened - average), axis=-1, keepdims=True)
    normed = ((widened - average) * lax.rsqrt(spread_sq + 1e-06) * ln_gain + ln_bias).astype(
        jnp.bfloat16
    )
    normed_v = normed.reshape(rows_here, n_y * n_zl, n_c, -1)
    normed_mine = lax.dynamic_index_in_dim(normed_v, c, axis=2, keepdims=False)
    normed_other = lax.dynamic_index_in_dim(normed_v, 1 - c, axis=2, keepdims=False)
    qkv_sums = (
        jnp.einsum("tjd,jdo->to", normed_mine, wq_mine, preferred_element_type=jnp.float32)
        + jnp.einsum("tjd,jdo->to", normed_other, wq_other, preferred_element_type=jnp.float32)
    ).reshape(rows_here, *w_qkv.shape[1:])
    row_ids = first_row + jnp.arange(rows_here, dtype=jnp.int32)
    segment, inside, is_patch, grid_row, grid_col, grid_side = layout_rows(
        row_ids, offsets, grids, row_count
    )
    query_matrix = rotate(qkv_sums[:, :, 0], is_patch, grid_row, grid_col, grid_side).astype(
        jnp.bfloat16
    )
    roped_keys = rotate(qkv_sums[:, :, 1], is_patch, grid_row, grid_col, grid_side).astype(
        jnp.bfloat16
    )
    values = qkv_sums[:, :, 2].astype(jnp.bfloat16)
    key_value = jnp.stack([roped_keys, values], axis=1)
    block_count = 2 * REACH + 1
    near = {0: key_value}
    for sign in (1, -1):
        odd = chain(key_value, SEQ, n_seq, sign)
        even = chain(key_value, SEQ, n_seq, 2 * sign)
        near[sign], near[2 * sign] = odd, even
        for distance in range(3, REACH + 1):
            if distance % 2:
                odd = chain(odd, SEQ, n_seq, 2 * sign)
                near[distance * sign] = odd
            else:
                even = chain(even, SEQ, n_seq, 2 * sign)
                near[distance * sign] = even
    kv_all = jnp.concatenate([near[d] for d in range(-REACH, REACH + 1)][::-1], axis=0)
    key_rows = first_row - REACH * rows_here + jnp.arange(block_count * rows_here, dtype=jnp.int32)
    key_layout = layout_rows(key_rows, offsets, grids, row_count)
    attended_output = attend_all(
        query_matrix, kv_all[:, 0], kv_all[:, 1], segment, inside, key_layout[0], key_layout[1]
    )
    wo_by_target = wo_full.reshape(*wo_full.shape[:2], n_zh, n_x, -1)
    by_target = jnp.einsum(
        "thf,hfzxd->xtzd", attended_output, wo_by_target, preferred_element_type=jnp.float32
    ).astype(jnp.bfloat16)

    from_peers = lax.all_to_all(by_target, "x", 0, 0, tiled=True)
    total = jnp.sum(from_peers.astype(jnp.float32), axis=0)
    keep = lax.dynamic_index_in_dim(total, zh, axis=1, keepdims=False)
    give = lax.dynamic_index_in_dim(total, 1 - zh, axis=1, keepdims=False)
    head_share = keep + ring(give.astype(jnp.bfloat16), "zh", n_zh, 1).astype(jnp.float32)

    layer_out = (tokens.astype(jnp.float32) + layer_scale * head_share).astype(jnp.bfloat16)
    next_rows = chain(layer_out[:HALO], SEQ, n_seq, -1)
    extended = jnp.concatenate([layer_out, next_rows], axis=0)
    is_corner = is_patch & (grid_row % 2 == 0) & (grid_col % 2 == 0)
    local_ids = jnp.arange(rows_here, dtype=jnp.int32)
    corner_index = jnp.stack(
        [local_ids, local_ids + 1, local_ids + grid_side, local_ids + grid_side + 1], axis=1
    )
    corner_index = jnp.clip(corner_index, 0, extended.shape[0] - 1)
    merged = jnp.take(extended, corner_index, axis=0)
    return jnp.where(is_corner[:, None, None], merged, jnp.zeros_like(merged))


def solution(mesh):
    n_seq, n_tp = mesh.devices.shape
    n_c = 2
    n_y = 4
    n_zh = 2
    sizes = (n_y, n_seq // (n_y * n_c), n_c, n_zh, n_tp // n_zh)
    split = Mesh(mesh.devices.reshape(sizes), ("y", "zl", "c", "zh", "x"))
    placed = (
        P(SEQ, TP),
        P(),
        P(),
        P(SEQ, TP, None, None),
        P(TP, None, SEQ),
        P(TP),
        P(),
        P(),
    )
    return jax.shard_map(
        functools.partial(body, sizes),
        mesh=split,
        in_specs=placed,
        out_specs=P(SEQ, None, TP),
        check_vma=False,
    )
```
